256 devices in a mesh: tm: 16 (over y, z_hi, core), space: 16 (over x, z_lo).
Axes of the slice: x: 4, y: 4, z: 8 (z_hi: 2, z_lo: 4; z = z_hi * 4 + z_lo), core: 2. Of those that a mesh axis runs over, the one named last changes fastest.
Arguments:
- guess: float32 [16, 4, 64, 64, 128], P('tm', None, 'space'), may hold values from 0 to 1
- fibre: int32 [64, 64, 128], P('space'), may hold values from 0 to 2
- labels: int32 [64, 64, 128], P('space'), may hold values from 0 to 3
Outputs:
- end_state: float32 [16, 4, 64, 64, 128], P('tm', None, 'space')
The draws below stay inside these ranges and needn't reach their ends.
All inputs are finite; a program needn't handle non-finite values.
Results may differ from the reference program's by a relative error of at most 0.0003.
Values sent between devices are 32-bit elements; how exact they have to be, the bound alone decides.
No kernel may reach another device: no remote copies, remote signals or barrier semaphores. Data moves between devices by JAX's collectives and lax.ppermute only.
A program may use at most 64 MiB of HBM per device.

```python
import jax
import jax.numpy as jnp
from jax import lax

CY = 64
CZ = 128
ITERS = 3
FIELDS = 4
SLICES = 16
NX = 64


def place_ends(array, rng, smallest, high):
    shape = array.shape
    index_at = [jax.random.randint(jax.random.fold_in(rng, axis), (), 0, shape[axis]) for axis in range(len(shape))]
    array = array.at[tuple(index_at)].set(smallest)
    longest = shape.index(max(shape))
    index_at[longest] = (index_at[longest] + 1) % shape[longest]
    return array.at[tuple(index_at)].set(high)


def levels(stream_key, dims, split, smallest, top_value):
    factor_of, own = 1.0, jax.random.fold_in(stream_key, 6)
    for dim, parts in split:
        steps = jnp.exp(jax.random.uniform(jax.random.fold_in(own, dim), (parts,), jnp.float32, smallest / len(split), top_value / len(split)))
        factor_of = factor_of * jnp.repeat(steps, dims[dim] // parts).reshape([-1 if axis == dim else 1 for axis in range(len(dims))])
    return factor_of


def setup_inputs(seed: int = 0) -> dict:
    arg_keys = jax.random.split(jax.random.key(seed), 4)
    return {
        "guess": jnp.clip(1.0 * jax.random.uniform(arg_keys[0], (SLICES, FIELDS, NX, CY, CZ), jnp.float32) ** levels(arg_keys[0], (SLICES, FIELDS, NX, CY, CZ), ((0, 16), (2, 16)), -0.2, 0.2), 0.0, 1.0),
        "fibre": place_ends(jax.random.randint(arg_keys[1], (NX, CY, CZ), 0, 3), jax.random.fold_in(arg_keys[1], 1), 0, 2).astype(jnp.int32),
        "labels": place_ends(jax.random.randint(arg_keys[2], (NX, CY, CZ), 0, 4), jax.random.fold_in(arg_keys[2], 1), 0, 3).astype(jnp.int32),
    }


radau_nodes = [0.05710419611451768, 0.27684301363812383, 0.5835904323689168, 0.8602401356562195, 1.0]
slice_len = 0.6


def radau_table():
    table = []
    for m in range(5):
        row_values = []
        for j in range(5):
            polynom = [1.0]
            for i in range(5):
                if i != j:
                    factor = radau_nodes[j] - radau_nodes[i]
                    shifted = [0.0] + [value / factor for value in polynom]
                    scaled = [-radau_nodes[i] * value / factor for value in polynom] + [0.0]
                    polynom = [shifted[p] + scaled[p] for p in range(len(polynom) + 1)]
            integral = 0.0
            for p in range(len(polynom)):
                integral = integral + polynom[p] * radau_nodes[m] ** (p + 1) / (p + 1)
            row_values.append(integral)
        table.append(row_values)
    return table


def lookup(labels, values):
    total = jnp.zeros(labels.shape, jnp.float32)
    for level in range(len(values)):
        total = total + jnp.where(labels == level, values[level], 0.0).astype(jnp.float32)
    return total


def coefficients(fibre, labels):
    fast_g = lookup(labels, [4.0, 3.0, 3.5, 1.0])
    slow_g = lookup(labels, [0.6, 0.9, 0.75, 0.3])
    slow_tau = 4.0 * lookup(labels, [1.0, 1.5, 1.2, 3.0])
    conduct = [0.2 + 0.6 * (fibre == d).astype(jnp.float32) for d in range(3)]
    return fast_g, slow_g, slow_tau, conduct


def edge_pad(field, axis):
    size = field.shape[axis]
    low = lax.slice_in_dim(field, 0, 1, axis=axis)
    high = lax.slice_in_dim(field, size - 1, size, axis=axis)
    return jnp.concatenate([low, field, high], axis=axis)


def second(padded, axis):
    size = padded.shape[axis]
    upper = lax.slice_in_dim(padded, 2, size, axis=axis)
    lower = lax.slice_in_dim(padded, 0, size - 2, axis=axis)
    middle = lax.slice_in_dim(padded, 1, size - 1, axis=axis)
    return upper + lower - 2.0 * middle


def diffuse(padded_x, volts, conduct):
    lap = conduct[0] * second(padded_x, 1)
    lap = lap + conduct[1] * second(edge_pad(volts, 2), 2)
    lap = lap + conduct[2] * second(edge_pad(volts, 3), 3)
    return lap


def rates(states, lap, fast_g, slow_g, slow_tau):
    volt = states[:, 0]
    act = states[:, 1]
    inact = states[:, 2]
    slow = states[:, 3]
    current = fast_g * act * act * act * inact * (volt - 1.0) + slow_g * slow * (volt + 0.2) + 0.3 * (volt + 0.1)
    dvolt = lap - current
    dact = (jax.nn.sigmoid(8.0 * (volt - 0.2)) - act) / 0.5
    dinact = (jax.nn.sigmoid(-8.0 * (volt - 0.3)) - inact) / (1.0 + 3.0 * jax.nn.sigmoid(6.0 * (volt - 0.3)))
    dslow = (jax.nn.sigmoid(5.0 * (volt - 0.5)) - slow) / slow_tau
    return jnp.stack([dvolt, dact, dinact, dslow], axis=1)


def quadrature(start, derivs, row):
    total = row[0] * derivs[0]
    for j in range(1, 5):
        total = total + row[j] * derivs[j]
    return start + slice_len * total


def reference(guess, fibre, labels):
    table = radau_table()
    fast_g, slow_g, slow_tau, conduct = coefficients(fibre, labels)

    def one_slice(carry, item):
        start0, index = item
        start = start0
        nodes = jnp.stack([start0] * 5)
        ends = []
        for k in range(ITERS):
            volts = nodes[:, 0]
            lap = diffuse(edge_pad(volts, 1), volts, conduct)
            derivs = rates(nodes, lap, fast_g, slow_g, slow_tau)
            nodes = jnp.stack([quadrature(start, derivs, table[m]) for m in range(5)])
            if k < ITERS - 1:
                ends.append(nodes[4])
                start = jnp.where(index == 0, start0, carry[k])
        return jnp.stack(ends), nodes[4]

    init = jnp.zeros((ITERS - 1,) + guess.shape[1:], jnp.float32)
    slice_ids = jnp.arange(SLICES).astype(jnp.int32)
    final_carry, outputs = lax.scan(one_slice, init, (guess, slice_ids))
    return outputs
```

```python
import jax
import jax.numpy as jnp
from jax import lax
from jax.sharding import PartitionSpec as P

ITERS = 3


radau_nodes = [0.05710419611451768, 0.2768430136381238, 0.5835904323689168, 0.8602401356562195, 1.0]
slice_len = 0.6


def radau_table():
    table = []
    for m in range(5):
        row_values = []
        for j in range(5):
            polynom = [1.0]
            for i in range(5):
                if i != j:
                    factor = radau_nodes[j] - radau_nodes[i]
                    shifted = [0.0] + [value / factor for value in polynom]
                    scaled = [-radau_nodes[i] * value / factor for value in polynom] + [0.0]
                    polynom = [shifted[p] + scaled[p] for p in range(len(polynom) + 1)]
            integral = 0.0
            for p in range(len(polynom)):
                integral = integral + polynom[p] * radau_nodes[m] ** (p + 1) / (p + 1)
            row_values.append(integral)
        table.append(row_values)
    return table


def lookup(labels, values):
    total = jnp.zeros(labels.shape, jnp.float32)
    for level in range(len(values)):
        total = total + jnp.where(labels == level, values[level], 0.0).astype(jnp.float32)
    return total


def edge_pad(field, axis):
    size = field.shape[axis]
    low = lax.slice_in_dim(field, 0, 1, axis=axis)
    high = lax.slice_in_dim(field, size - 1, size, axis=axis)
    return jnp.concatenate([low, field, high], axis=axis)


def second(padded, axis):
    size = padded.shape[axis]
    upper = lax.slice_in_dim(padded, 2, size, axis=axis)
    lower = lax.slice_in_dim(padded, 0, size - 2, axis=axis)
    middle = lax.slice_in_dim(padded, 1, size - 1, axis=axis)
    return upper + lower - 2.0 * middle


def shift_space(block, forward):
    count = lax.axis_size("space")
    pairs = [(i, i + 1) for i in range(count - 1)]
    if not forward:
        pairs = [(t, s) for s, t in pairs]
    return lax.ppermute(block, "space", pairs)


def halos(volts):
    planes = volts.shape[-3]
    low = shift_space(volts[..., planes - 1 : planes, :, :], True)
    high = shift_space(volts[..., 0:1, :, :], False)
    return low, high


def laplacian(volts, low, high, conduct):
    padded = jnp.concatenate([low, volts, high], axis=-3)
    lap = conduct[0] * second(padded, volts.ndim - 3)
    lap = lap + conduct[1] * second(edge_pad(volts, volts.ndim - 2), volts.ndim - 2)
    lap = lap + conduct[2] * second(edge_pad(volts, volts.ndim - 1), volts.ndim - 1)
    return lap


def rates(states, lap, fast_g, slow_g, slow_tau):
    volt = states[..., 0, :, :, :]
    act = states[..., 1, :, :, :]
    inact = states[..., 2, :, :, :]
    slow = states[..., 3, :, :, :]
    current = (
        fast_g * act * act * act * inact * (volt - 1.0)
        + slow_g * slow * (volt + 0.2)
        + 0.3 * (volt + 0.1)
    )
    dvolt = lap - current
    dact = (jax.nn.sigmoid(8.0 * (volt - 0.2)) - act) / 0.5
    dinact = (jax.nn.sigmoid(-8.0 * (volt - 0.3)) - inact) / (
        1.0 + 3.0 * jax.nn.sigmoid(6.0 * (volt - 0.3))
    )
    dslow = (jax.nn.sigmoid(5.0 * (volt - 0.5)) - slow) / slow_tau
    return jnp.stack([dvolt, dact, dinact, dslow], axis=-4)


def quadrature(start, derivs, row):
    total = row[0] * derivs[0]
    for j in range(1, 5):
        total = total + row[j] * derivs[j]
    return start + slice_len * total


def shards(guess, fibre, labels):
    table = radau_table()
    sums = [sum(row) for row in table]
    fast_g = lookup(labels, [4.0, 3.0, 3.5, 1.0])
    slow_g = lookup(labels, [0.6, 0.9, 0.75, 0.3])
    slow_tau = 4.0 * lookup(labels, [1.0, 1.5, 1.2, 3.0])
    conduct = [0.2 + 0.6 * (fibre == d).astype(jnp.float32) for d in range(3)]
    place = lax.axis_index("space")
    at_low = place == 0
    at_high = place == lax.axis_size("space") - 1
    first_slice = lax.axis_index("tm") == 0
    count = lax.axis_size("tm")
    tm_pairs = [(i, i + 1) for i in range(count - 1)]

    start0 = guess[0]
    volts0 = start0[0]
    planes = volts0.shape[0]

    low0, high0 = halos(volts0)
    low0 = jnp.where(at_low, volts0[:1], low0)
    high0 = jnp.where(at_high, volts0[planes - 1 :], high0)
    derivs0 = rates(start0, laplacian(volts0, low0, high0, conduct), fast_g, slow_g, slow_tau)
    ends0 = start0 + slice_len * (sums[4] * derivs0)
    arrived1 = lax.ppermute(ends0, "tm", tm_pairs)

    dv = derivs0[0]
    dlow, dhigh = halos(dv)
    nodes0 = jnp.stack([start0 + slice_len * (sums[m] * derivs0) for m in range(5)])
    volts1 = nodes0[:, 0]
    low1 = jnp.stack([low0 + slice_len * (sums[m] * dlow) for m in range(5)])
    high1 = jnp.stack([high0 + slice_len * (sums[m] * dhigh) for m in range(5)])
    low1 = jnp.where(at_low, volts1[:, :1], low1)
    high1 = jnp.where(at_high, volts1[:, planes - 1 :], high1)
    derivs1 = rates(nodes0, laplacian(volts1, low1, high1, conduct), fast_g, slow_g, slow_tau)
    start1 = jnp.where(first_slice, start0, arrived1)
    ends1 = quadrature(start1, derivs1, table[4])
    arrived2 = lax.ppermute(ends1, "tm", tm_pairs)
    nodes1 = jnp.stack([quadrature(start1, derivs1, table[m]) for m in range(4)] + [ends1])

    volts2 = nodes1[:, 0]
    low2, high2 = halos(volts2)
    low2 = jnp.where(at_low, volts2[:, :1], low2)
    high2 = jnp.where(at_high, volts2[:, planes - 1 :], high2)
    derivs2 = rates(nodes1, laplacian(volts2, low2, high2, conduct), fast_g, slow_g, slow_tau)
    start2 = jnp.where(first_slice, start0, arrived2)
    ends2 = quadrature(start2, derivs2, table[4])
    return ends2[None]


def solution(mesh):
    placed = (P("tm", None, "space", None, None), P("space", None, None), P("space", None, None))
    return jax.shard_map(
        shards,
        mesh=mesh,
        in_specs=placed,
        out_specs=P("tm", None, "space", None, None),
        check_vma=False,
    )
```

```python
import jax
import jax.numpy as jnp
from jax import lax
from jax.sharding import PartitionSpec as P


radau_nodes = [0.05710419611451768, 0.2768430136381238, 0.5835904323689168, 0.8602401356562195, 1.0]
slice_len = 0.6


def radau_table():
    table = []
    for m in range(5):
        row_values = []
        for j in range(5):
            polynom = [1.0]
            for i in range(5):
                if i != j:
                    factor = radau_nodes[j] - radau_nodes[i]
                    shifted = [0.0] + [value / factor for value in polynom]
                    scaled = [-radau_nodes[i] * value / factor for value in polynom] + [0.0]
                    polynom = [shifted[p] + scaled[p] for p in range(len(polynom) + 1)]
            integral = 0.0
            for p in range(len(polynom)):
                integral = integral + polynom[p] * radau_nodes[m] ** (p + 1) / (p + 1)
            row_values.append(integral)
        table.append(row_values)
    return table


def lookup(labels, values):
    total = jnp.zeros(labels.shape, jnp.float32)
    for level in range(len(values)):
        total = total + jnp.where(labels == level, values[level], 0.0).astype(jnp.float32)
    return total


def edge_pad(field, axis):
    size = field.shape[axis]
    low = lax.slice_in_dim(field, 0, 1, axis=axis)
    high = lax.slice_in_dim(field, size - 1, size, axis=axis)
    return jnp.concatenate([low, field, high], axis=axis)


def second(padded, axis):
    size = padded.shape[axis]
    upper = lax.slice_in_dim(padded, 2, size, axis=axis)
    lower = lax.slice_in_dim(padded, 0, size - 2, axis=axis)
    middle = lax.slice_in_dim(padded, 1, size - 1, axis=axis)
    return upper + lower - 2.0 * middle


def shift_space(block, forward):
    count = lax.axis_size("space")
    pairs = [(i, i + 1) for i in range(count - 1)]
    if not forward:
        pairs = [(t, s) for s, t in pairs]
    return lax.ppermute(block, "space", pairs)


def halos(volts):
    planes = volts.shape[-3]
    low = shift_space(volts[..., planes - 1 : planes, :, :], True)
    high = shift_space(volts[..., 0:1, :, :], False)
    return low, high


def laplacian(volts, low, high, conduct):
    padded = jnp.concatenate([low, volts, high], axis=-3)
    lap = conduct[0] * second(padded, volts.ndim - 3)
    lap = lap + conduct[1] * second(edge_pad(volts, volts.ndim - 2), volts.ndim - 2)
    lap = lap + conduct[2] * second(edge_pad(volts, volts.ndim - 1), volts.ndim - 1)
    return lap


def rates(states, lap, fast_g, slow_g, slow_tau):
    volt = states[..., 0, :, :, :]
    act = states[..., 1, :, :, :]
    inact = states[..., 2, :, :, :]
    slow = states[..., 3, :, :, :]
    current = (
        fast_g * act * act * act * inact * (volt - 1.0)
        + slow_g * slow * (volt + 0.2)
        + 0.3 * (volt + 0.1)
    )
    dvolt = lap - current
    dact = (jax.nn.sigmoid(8.0 * (volt - 0.2)) - act) / 0.5
    dinact = (jax.nn.sigmoid(-8.0 * (volt - 0.3)) - inact) / (
        1.0 + 3.0 * jax.nn.sigmoid(6.0 * (volt - 0.3))
    )
    dslow = (jax.nn.sigmoid(5.0 * (volt - 0.5)) - slow) / slow_tau
    return jnp.stack([dvolt, dact, dinact, dslow], axis=-4)


def quadrature(start, derivs, row):
    total = row[0] * derivs[0]
    for j in range(1, 5):
        total = total + row[j] * derivs[j]
    return start + slice_len * total


def steps(guess, fibre, labels):
    table = radau_table()
    sums = [sum(row) for row in table]
    fast_g = lookup(labels, [4.0, 3.0, 3.5, 1.0])
    slow_g = lookup(labels, [0.6, 0.9, 0.75, 0.3])
    slow_tau = 4.0 * lookup(labels, [1.0, 1.5, 1.2, 3.0])
    conduct = [0.2 + 0.6 * (fibre == d).astype(jnp.float32) for d in range(3)]
    place = lax.axis_index("space")
    at_low = place == 0
    at_high = place == lax.axis_size("space") - 1
    first_slice = lax.axis_index("tm") == 0
    count = lax.axis_size("tm")
    tm_pairs = [(i, i + 1) for i in range(count - 1)]

    start0 = guess[0]
    volts0 = start0[0]
    planes = volts0.shape[0]

    rough = rates(start0, laplacian(volts0, volts0[:1], volts0[planes - 1 :], conduct), fast_g, slow_g, slow_tau)
    rough_ends, edge_volts = lax.optimization_barrier((start0 + slice_len * (sums[4] * rough), volts0))
    arrived_rough = lax.ppermute(rough_ends, "tm", tm_pairs)
    low0, high0 = halos(edge_volts)
    low0 = jnp.where(at_low, volts0[:1], low0)
    high0 = jnp.where(at_high, volts0[planes - 1 :], high0)
    derivs0 = rates(start0, laplacian(volts0, low0, high0, conduct), fast_g, slow_g, slow_tau)
    ends0 = start0 + slice_len * (sums[4] * derivs0)
    edges = jnp.concatenate([ends0[0, :1], ends0[0, planes - 1 :]])
    arrived_edges = lax.ppermute(edges, "tm", tm_pairs)
    arrived1 = arrived_rough.at[0, 0].set(arrived_edges[0]).at[0, planes - 1].set(arrived_edges[1])

    dv = derivs0[0]
    dlow, dhigh = halos(dv)
    nodes0 = jnp.stack([start0 + slice_len * (sums[m] * derivs0) for m in range(5)])
    volts1 = nodes0[:, 0]
    low1 = jnp.stack([low0 + slice_len * (sums[m] * dlow) for m in range(5)])
    high1 = jnp.stack([high0 + slice_len * (sums[m] * dhigh) for m in range(5)])
    low1 = jnp.where(at_low, volts1[:, :1], low1)
    high1 = jnp.where(at_high, volts1[:, planes - 1 :], high1)
    derivs1 = rates(nodes0, laplacian(volts1, low1, high1, conduct), fast_g, slow_g, slow_tau)
    start1 = jnp.where(first_slice, start0, arrived1)
    ends1 = quadrature(start1, derivs1, table[4])
    arrived2 = lax.ppermute(ends1, "tm", tm_pairs)
    nodes1 = jnp.stack([quadrature(start1, derivs1, table[m]) for m in range(4)] + [ends1])

    volts2 = nodes1[:, 0]
    low2, high2 = halos(volts2)
    low2 = jnp.where(at_low, volts2[:, :1], low2)
    high2 = jnp.where(at_high, volts2[:, planes - 1 :], high2)
    derivs2 = rates(nodes1, laplacian(volts2, low2, high2, conduct), fast_g, slow_g, slow_tau)
    start2 = jnp.where(first_slice, start0, arrived2)
    ends2 = quadrature(start2, derivs2, table[4])
    return ends2[None]


def solution(mesh):
    placed = (P("tm", None, "space", None, None), P("space", None, None), P("space", None, None))
    return jax.shard_map(
        steps,
        mesh=mesh,
        in_specs=placed,
        out_specs=P("tm", None, "space", None, None),
        check_vma=False,
    )
```

```python
import jax
import jax.numpy as jnp
from jax import lax
from jax.sharding import PartitionSpec as P

ITERS = 3


radau_nodes = [0.05710419611451768, 0.2768430136381238, 0.5835904323689168, 0.8602401356562195, 1.0]
slice_len = 0.6


def radau_table():
    table = []
    for m in range(5):
        row_values = []
        for j in range(5):
            polynom = [1.0]
            for i in range(5):
                if i != j:
                    factor = radau_nodes[j] - radau_nodes[i]
                    shifted = [0.0] + [value / factor for value in polynom]
                    scaled = [-radau_nodes[i] * value / factor for value in polynom] + [0.0]
                    polynom = [shifted[p] + scaled[p] for p in range(len(polynom) + 1)]
            integral = 0.0
            for p in range(len(polynom)):
                integral = integral + polynom[p] * radau_nodes[m] ** (p + 1) / (p + 1)
            row_values.append(integral)
        table.append(row_values)
    return table


def lookup(labels, values):
    total = jnp.zeros(labels.shape, jnp.float32)
    for level in range(len(values)):
        total = total + jnp.where(labels == level, values[level], 0.0).astype(jnp.float32)
    return total


def edge_pad(field, axis):
    size = field.shape[axis]
    low = lax.slice_in_dim(field, 0, 1, axis=axis)
    high = lax.slice_in_dim(field, size - 1, size, axis=axis)
    return jnp.concatenate([low, field, high], axis=axis)


def second(padded, axis):
    size = padded.shape[axis]
    upper = lax.slice_in_dim(padded, 2, size, axis=axis)
    lower = lax.slice_in_dim(padded, 0, size - 2, axis=axis)
    middle = lax.slice_in_dim(padded, 1, size - 1, axis=axis)
    return upper + lower - 2.0 * middle


def shift_space(block, forward):
    count = lax.axis_size("space")
    pairs = [(i, i + 1) for i in range(count - 1)]
    if not forward:
        pairs = [(t, s) for s, t in pairs]
    return lax.ppermute(block, "space", pairs)


def close_edges(volts, depth, at_low, at_high):
    size = volts.shape[-3]
    inner_low = volts[..., depth : depth + 1, :, :]
    inner_high = volts[..., size - depth - 1 : size - depth, :, :]
    outer_low = jnp.where(at_low, inner_low, volts[..., depth - 1 : depth, :, :])
    outer_high = jnp.where(at_high, inner_high, volts[..., size - depth : size - depth + 1, :, :])
    return jnp.concatenate(
        [volts[..., : depth - 1, :, :], outer_low, volts[..., depth : size - depth, :, :], outer_high,
         volts[..., size - depth + 1 :, :, :]],
        axis=-3,
    )


def laplacian(volts, conduct):
    x = volts.ndim - 3
    inner = lax.slice_in_dim(volts, 1, volts.shape[x] - 1, axis=x)
    lap = conduct[0] * second(volts, x)
    lap = lap + conduct[1] * second(edge_pad(inner, x + 1), x + 1)
    lap = lap + conduct[2] * second(edge_pad(inner, x + 2), x + 2)
    return lap


def rates(states, lap, fast_g, slow_g, slow_tau):
    volt = states[..., 0, :, :, :]
    act = states[..., 1, :, :, :]
    inact = states[..., 2, :, :, :]
    slow = states[..., 3, :, :, :]
    current = (
        fast_g * act * act * act * inact * (volt - 1.0)
        + slow_g * slow * (volt + 0.2)
        + 0.3 * (volt + 0.1)
    )
    dvolt = lap - current
    dact = (jax.nn.sigmoid(8.0 * (volt - 0.2)) - act) / 0.5
    dinact = (jax.nn.sigmoid(-8.0 * (volt - 0.3)) - inact) / (
        1.0 + 3.0 * jax.nn.sigmoid(6.0 * (volt - 0.3))
    )
    dslow = (jax.nn.sigmoid(5.0 * (volt - 0.5)) - slow) / slow_tau
    return jnp.stack([dvolt, dact, dinact, dslow], axis=-4)


def quadrature(start, derivs, row):
    total = row[0] * derivs[0]
    for j in range(1, 5):
        total = total + row[j] * derivs[j]
    return start + slice_len * total


def trim(block, depth):
    size = block.shape[-3]
    return block[..., depth : size - depth, :, :]


def shards(guess, fibre, labels):
    table = radau_table()
    sums = [sum(row) for row in table]
    place = lax.axis_index("space")
    at_low = place == 0
    at_high = place == lax.axis_size("space") - 1
    first_slice = lax.axis_index("tm") == 0
    count = lax.axis_size("tm")
    tm_pairs = [(i, i + 1) for i in range(count - 1)]

    start0 = guess[0]
    planes = start0.shape[1]
    code = (labels + 4 * fibre).astype(jnp.float32)

    top = jnp.concatenate([start0[0, planes - 3 :], start0[1:, planes - 2 :].reshape(-1, *start0.shape[2:]), code[planes - 2 :]])
    bottom = jnp.concatenate([start0[0, :3], start0[1:, :2].reshape(-1, *start0.shape[2:]), code[:2]])
    below = shift_space(top, True)
    above = shift_space(bottom, False)

    def unpack(part, volts_first):
        volts = part[:3]
        gates = part[3:9].reshape(3, 2, *part.shape[1:])
        return volts, gates, part[9:11]

    low_v, low_g, low_c = unpack(below, True)
    high_v, high_g, high_c = unpack(above, False)
    volts_ext = jnp.concatenate([low_v, start0[0], high_v])
    gates_ext = jnp.concatenate([low_g, start0[1:], high_g], axis=1)
    code_ext = jnp.concatenate([low_c, code, high_c]).astype(jnp.int32)
    fibre_ext = code_ext // 4
    labels_ext = code_ext % 4
    fast_g = lookup(labels_ext, [4.0, 3.0, 3.5, 1.0])
    slow_g = lookup(labels_ext, [0.6, 0.9, 0.75, 0.3])
    slow_tau = 4.0 * lookup(labels_ext, [1.0, 1.5, 1.2, 3.0])
    conduct = [0.2 + 0.6 * (fibre_ext == d).astype(jnp.float32) for d in range(3)]
    coef = lambda depth: [trim(c, 2 - depth) for c in (fast_g, slow_g, slow_tau)]
    cond = lambda depth: [trim(c, 2 - depth) for c in conduct]

    state_ext = jnp.concatenate([trim(volts_ext, 1)[None], gates_ext])
    lap0 = laplacian(close_edges(volts_ext, 3, at_low, at_high), cond(2))
    derivs0 = rates(state_ext, lap0, *coef(2))
    nodes0 = jnp.stack([state_ext + slice_len * (sums[m] * derivs0) for m in range(5)])
    ends0 = trim(nodes0[4], 1)
    message1 = jnp.concatenate(
        [trim(ends0, 1).reshape(-1, *ends0.shape[2:]), ends0[0, :1], ends0[0, planes + 1 :]]
    )
    arrived1 = lax.ppermute(message1, "tm", tm_pairs)
    fields = start0.shape[0]
    start1_block = jnp.where(first_slice, start0, arrived1[: fields * planes].reshape(start0.shape))
    start1_volts = jnp.where(
        first_slice,
        trim(volts_ext, 2),
        jnp.concatenate([arrived1[fields * planes : fields * planes + 1], start1_block[0], arrived1[fields * planes + 1 :]]),
    )

    lap1 = laplacian(close_edges(nodes0[:, 0], 2, at_low, at_high), cond(1))
    derivs1 = rates(trim(nodes0, 1), lap1, *coef(1))
    ends1 = quadrature(start1_block, trim(derivs1, 1), table[4])
    arrived2 = lax.ppermute(ends1, "tm", tm_pairs)
    volts1 = jnp.stack([quadrature(start1_volts, derivs1[:, 0], table[m]) for m in range(5)])
    gates1 = jnp.stack([quadrature(start1_block[1:], trim(derivs1[:, 1:], 1), table[m]) for m in range(5)])
    nodes1 = jnp.concatenate([trim(volts1, 1)[:, None], gates1], axis=1)

    lap2 = laplacian(close_edges(volts1, 1, at_low, at_high), cond(0))
    derivs2 = rates(nodes1, lap2, *coef(0))
    start2 = jnp.where(first_slice, start0, arrived2)
    ends2 = quadrature(start2, derivs2, table[4])
    return ends2[None]


def solution(mesh):
    placed = (P("tm", None, "space", None, None), P("space", None, None), P("space", None, None))
    return jax.shard_map(
        shards,
        mesh=mesh,
        in_specs=placed,
        out_specs=P("tm", None, "space", None, None),
        check_vma=False,
    )
```

```python
import jax
import jax.numpy as jnp
from jax import lax
from jax.sharding import PartitionSpec as P


radau_nodes = [0.05710419611451768, 0.2768430136381238, 0.5835904323689168, 0.8602401356562195, 1.0]
slice_len = 0.6


def radau_table():
    table = []
    for m in range(5):
        row_values = []
        for j in range(5):
            polynom = [1.0]
            for i in range(5):
                if i != j:
                    factor = radau_nodes[j] - radau_nodes[i]
                    shifted = [0.0] + [value / factor for value in polynom]
                    scaled = [-radau_nodes[i] * value / factor for value in polynom] + [0.0]
                    polynom = [shifted[p] + scaled[p] for p in range(len(polynom) + 1)]
            integral = 0.0
            for p in range(len(polynom)):
                integral = integral + polynom[p] * radau_nodes[m] ** (p + 1) / (p + 1)
            row_values.append(integral)
        table.append(row_values)
    return table


def lookup(labels, values):
    total = jnp.zeros(labels.shape, jnp.float32)
    for level in range(len(values)):
        total = total + jnp.where(labels == level, values[level], 0.0).astype(jnp.float32)
    return total


def edge_pad(field, axis):
    size = field.shape[axis]
    low = lax.slice_in_dim(field, 0, 1, axis=axis)
    high = lax.slice_in_dim(field, size - 1, size, axis=axis)
    return jnp.concatenate([low, field, high], axis=axis)


def second(padded, axis):
    size = padded.shape[axis]
    upper = lax.slice_in_dim(padded, 2, size, axis=axis)
    lower = lax.slice_in_dim(padded, 0, size - 2, axis=axis)
    middle = lax.slice_in_dim(padded, 1, size - 1, axis=axis)
    return upper + lower - 2.0 * middle


def shift_space(block, forward):
    count = lax.axis_size("space")
    pairs = [(i, i + 1) for i in range(count - 1)]
    if not forward:
        pairs = [(t, s) for s, t in pairs]
    return lax.ppermute(block, "space", pairs)


def halos(volts):
    planes = volts.shape[-3]
    low = shift_space(volts[..., planes - 1 : planes, :, :], True)
    high = shift_space(volts[..., 0:1, :, :], False)
    return low, high


def laplacian(volts, low, high, conduct):
    padded = jnp.concatenate([low, volts, high], axis=-3)
    lap = conduct[0] * second(padded, volts.ndim - 3)
    lap = lap + conduct[1] * second(edge_pad(volts, volts.ndim - 2), volts.ndim - 2)
    lap = lap + conduct[2] * second(edge_pad(volts, volts.ndim - 1), volts.ndim - 1)
    return lap


def rates(states, lap, fast_g, slow_g, slow_tau):
    volt = states[..., 0, :, :, :]
    act = states[..., 1, :, :, :]
    inact = states[..., 2, :, :, :]
    slow = states[..., 3, :, :, :]
    current = (
        fast_g * act * act * act * inact * (volt - 1.0)
        + slow_g * slow * (volt + 0.2)
        + 0.3 * (volt + 0.1)
    )
    dvolt = lap - current
    dact = (jax.nn.sigmoid(8.0 * (volt - 0.2)) - act) / 0.5
    dinact = (jax.nn.sigmoid(-8.0 * (volt - 0.3)) - inact) / (
        1.0 + 3.0 * jax.nn.sigmoid(6.0 * (volt - 0.3))
    )
    dslow = (jax.nn.sigmoid(5.0 * (volt - 0.5)) - slow) / slow_tau
    return jnp.stack([dvolt, dact, dinact, dslow], axis=-4)


def quadrature(start, derivs, row):
    total = row[0] * derivs[0]
    for j in range(1, 5):
        total = total + row[j] * derivs[j]
    return start + slice_len * total


def steps(guess, fibre, labels):
    table = radau_table()
    sums = [sum(row) for row in table]
    fast_g = lookup(labels, [4.0, 3.0, 3.5, 1.0])
    slow_g = lookup(labels, [0.6, 0.9, 0.75, 0.3])
    slow_tau = 4.0 * lookup(labels, [1.0, 1.5, 1.2, 3.0])
    conduct = [0.2 + 0.6 * (fibre == d).astype(jnp.float32) for d in range(3)]
    place = lax.axis_index("space")
    at_low = place == 0
    at_high = place == lax.axis_size("space") - 1
    first_slice = lax.axis_index("tm") == 0
    count = lax.axis_size("tm")
    tm_pairs = [(i, i + 1) for i in range(count - 1)]

    start0 = guess[0]
    volts0 = start0[0]
    planes = volts0.shape[0]

    low0, high0 = halos(volts0)
    low0 = jnp.where(at_low, volts0[:1], low0)
    high0 = jnp.where(at_high, volts0[planes - 1 :], high0)
    derivs0 = rates(start0, laplacian(volts0, low0, high0, conduct), fast_g, slow_g, slow_tau)
    ends0 = start0 + slice_len * (sums[4] * derivs0)
    arrived1 = lax.ppermute(ends0, "tm", tm_pairs)

    dv = derivs0[0]
    dlow, dhigh = halos(dv)
    nodes0 = jnp.stack([start0 + slice_len * (sums[m] * derivs0) for m in range(5)])
    volts1 = nodes0[:, 0]
    low1 = jnp.stack([low0 + slice_len * (sums[m] * dlow) for m in range(5)])
    high1 = jnp.stack([high0 + slice_len * (sums[m] * dhigh) for m in range(5)])
    low1 = jnp.where(at_low, volts1[:, :1], low1)
    high1 = jnp.where(at_high, volts1[:, planes - 1 :], high1)
    derivs1 = rates(nodes0, laplacian(volts1, low1, high1, conduct), fast_g, slow_g, slow_tau)
    start1 = jnp.where(first_slice, start0, arrived1)
    ends1 = quadrature(start1, derivs1, table[4])
    arrived2 = lax.ppermute(ends1, "tm", tm_pairs)
    nodes1 = jnp.stack([quadrature(start1, derivs1, table[m]) for m in range(4)] + [ends1])

    volts2 = nodes1[:, 0]
    low2, high2 = halos(volts2)
    low2 = jnp.where(at_low, volts2[:, :1], low2)
    high2 = jnp.where(at_high, volts2[:, planes - 1 :], high2)
    derivs2 = rates(nodes1, laplacian(volts2, low2, high2, conduct), fast_g, slow_g, slow_tau)
    start2 = jnp.where(first_slice, start0, arrived2)
    ends2 = quadrature(start2, derivs2, table[4])
    return ends2[None]


def solution(mesh):
    placed = (P("tm", None, "space", None, None), P("space", None, None), P("space", None, None))
    return jax.shard_map(
        steps,
        mesh=mesh,
        in_specs=placed,
        out_specs=P("tm", None, "space", None, None),
        check_vma=False,
    )
```

```python
import jax
import jax.numpy as jnp
from jax import lax
from jax.sharding import PartitionSpec as P


radau_nodes = [0.05710419611451768, 0.2768430136381238, 0.5835904323689168, 0.8602401356562195, 1.0]
slice_len = 0.6


def radau_table():
    table = []
    for m in range(5):
        row_values = []
        for j in range(5):
            polynom = [1.0]
            for i in range(5):
                if i != j:
                    factor = radau_nodes[j] - radau_nodes[i]
                    shifted = [0.0] + [value / factor for value in polynom]
                    scaled = [-radau_nodes[i] * value / factor for value in polynom] + [0.0]
                    polynom = [shifted[p] + scaled[p] for p in range(len(polynom) + 1)]
            integral = 0.0
            for p in range(len(polynom)):
                integral = integral + polynom[p] * radau_nodes[m] ** (p + 1) / (p + 1)
            row_values.append(integral)
        table.append(row_values)
    return table


def lookup(labels, values):
    total = jnp.zeros(labels.shape, jnp.float32)
    for level in range(len(values)):
        total = total + jnp.where(labels == level, values[level], 0.0).astype(jnp.float32)
    return total


def edge_pad(field, axis):
    size = field.shape[axis]
    low = lax.slice_in_dim(field, 0, 1, axis=axis)
    high = lax.slice_in_dim(field, size - 1, size, axis=axis)
    return jnp.concatenate([low, field, high], axis=axis)


def second(padded, axis):
    size = padded.shape[axis]
    upper = lax.slice_in_dim(padded, 2, size, axis=axis)
    lower = lax.slice_in_dim(padded, 0, size - 2, axis=axis)
    middle = lax.slice_in_dim(padded, 1, size - 1, axis=axis)
    return upper + lower - 2.0 * middle


def shift_space(block, forward):
    count = lax.axis_size("space")
    pairs = [(i, i + 1) for i in range(count - 1)]
    if not forward:
        pairs = [(t, s) for s, t in pairs]
    return lax.ppermute(block, "space", pairs)


def halos(volts):
    planes = volts.shape[-3]
    low = shift_space(volts[..., planes - 1 : planes, :, :], True)
    high = shift_space(volts[..., 0:1, :, :], False)
    return low, high


def laplacian(volts, low, high, conduct):
    padded = jnp.concatenate([low, volts, high], axis=-3)
    lap = conduct[0] * second(padded, volts.ndim - 3)
    lap = lap + conduct[1] * second(edge_pad(volts, volts.ndim - 2), volts.ndim - 2)
    lap = lap + conduct[2] * second(edge_pad(volts, volts.ndim - 1), volts.ndim - 1)
    return lap


def rates(states, lap, fast_g, slow_g, slow_tau):
    volt = states[..., 0, :, :, :]
    act = states[..., 1, :, :, :]
    inact = states[..., 2, :, :, :]
    slow = states[..., 3, :, :, :]
    current = (
        fast_g * act * act * act * inact * (volt - 1.0)
        + slow_g * slow * (volt + 0.2)
        + 0.3 * (volt + 0.1)
    )
    dvolt = lap - current
    dact = (jax.nn.sigmoid(8.0 * (volt - 0.2)) - act) / 0.5
    dinact = (jax.nn.sigmoid(-8.0 * (volt - 0.3)) - inact) / (
        1.0 + 3.0 * jax.nn.sigmoid(6.0 * (volt - 0.3))
    )
    dslow = (jax.nn.sigmoid(5.0 * (volt - 0.5)) - slow) / slow_tau
    return jnp.stack([dvolt, dact, dinact, dslow], axis=-4)


def quadrature(start, derivs, row):
    total = row[0] * derivs[0]
    for j in range(1, 5):
        total = total + row[j] * derivs[j]
    return start + slice_len * total


def edge_nodes(start, derivs, weights):
    total = weights[:, 0] * derivs[0][None]
    for j in range(1, 5):
        total = total + weights[:, j] * derivs[j][None]
    return start[None] + slice_len * total


def steps(guess, fibre, labels):
    table = radau_table()
    sums = [sum(row) for row in table]
    fast_g = lookup(labels, [4.0, 3.0, 3.5, 1.0])
    slow_g = lookup(labels, [0.6, 0.9, 0.75, 0.3])
    slow_tau = 4.0 * lookup(labels, [1.0, 1.5, 1.2, 3.0])
    conduct = [0.2 + 0.6 * (fibre == d).astype(jnp.float32) for d in range(3)]
    place = lax.axis_index("space")
    at_low = place == 0
    at_high = place == lax.axis_size("space") - 1
    first_slice = lax.axis_index("tm") == 0
    count = lax.axis_size("tm")
    tm_pairs = [(i, i + 1) for i in range(count - 1)]

    start0 = guess[0]
    volts0 = start0[0]
    planes = volts0.shape[0]

    low0, high0 = halos(volts0)
    low0 = jnp.where(at_low, volts0[:1], low0)
    high0 = jnp.where(at_high, volts0[planes - 1 :], high0)
    derivs0 = rates(start0, laplacian(volts0, low0, high0, conduct), fast_g, slow_g, slow_tau)
    ends0 = start0 + slice_len * (sums[4] * derivs0)
    arrived1 = lax.ppermute(ends0, "tm", tm_pairs)

    dv = derivs0[0]
    dlow, dhigh = halos(dv)
    nodes0 = jnp.stack([start0 + slice_len * (sums[m] * derivs0) for m in range(5)])
    volts1 = nodes0[:, 0]
    low1 = jnp.stack([low0 + slice_len * (sums[m] * dlow) for m in range(5)])
    high1 = jnp.stack([high0 + slice_len * (sums[m] * dhigh) for m in range(5)])
    low1 = jnp.where(at_low, volts1[:, :1], low1)
    high1 = jnp.where(at_high, volts1[:, planes - 1 :], high1)
    derivs1 = rates(nodes0, laplacian(volts1, low1, high1, conduct), fast_g, slow_g, slow_tau)
    start1 = jnp.where(first_slice, start0, arrived1)
    ends1 = quadrature(start1, derivs1, table[4])
    arrived2 = lax.ppermute(ends1, "tm", tm_pairs)
    weights = jnp.array(table, jnp.float32)[:, :, None, None, None]
    top = edge_nodes(start1[0, planes - 1 :], derivs1[:, 0, planes - 1 :], weights)
    bottom = edge_nodes(start1[0, :1], derivs1[:, 0, :1], weights)
    low2 = shift_space(top, True)
    high2 = shift_space(bottom, False)
    later_start, later_derivs, ends1 = lax.optimization_barrier((start1, derivs1, ends1))
    nodes1 = jnp.stack([quadrature(later_start, later_derivs, table[m]) for m in range(4)] + [ends1])

    volts2 = nodes1[:, 0]
    low2 = jnp.where(at_low, volts2[:, :1], low2)
    high2 = jnp.where(at_high, volts2[:, planes - 1 :], high2)
    derivs2 = rates(nodes1, laplacian(volts2, low2, high2, conduct), fast_g, slow_g, slow_tau)
    start2 = jnp.where(first_slice, start0, arrived2)
    ends2 = quadrature(start2, derivs2, table[4])
    return ends2[None]


def solution(mesh):
    placed = (P("tm", None, "space", None, None), P("space", None, None), P("space", None, None))
    return jax.shard_map(
        steps,
        mesh=mesh,
        in_specs=placed,
        out_specs=P("tm", None, "space", None, None),
        check_vma=False,
    )
```

```python
import jax
import jax.numpy as jnp
from jax import lax
from jax.sharding import PartitionSpec as P


radau_nodes = [0.05710419611451768, 0.2768430136381238, 0.5835904323689168, 0.8602401356562195, 1.0]
slice_len = 0.6


def radau_table():
    table = []
    for m in range(5):
        row_values = []
        for j in range(5):
            polynom = [1.0]
            for i in range(5):
                if i != j:
                    factor = radau_nodes[j] - radau_nodes[i]
                    shifted = [0.0] + [value / factor for value in polynom]
                    scaled = [-radau_nodes[i] * value / factor for value in polynom] + [0.0]
                    polynom = [shifted[p] + scaled[p] for p in range(len(polynom) + 1)]
            integral = 0.0
            for p in range(len(polynom)):
                integral = integral + polynom[p] * radau_nodes[m] ** (p + 1) / (p + 1)
            row_values.append(integral)
        table.append(row_values)
    return table


def lookup(labels, values):
    total = jnp.zeros(labels.shape, jnp.float32)
    for level in range(len(values)):
        total = total + jnp.where(labels == level, values[level], 0.0).astype(jnp.float32)
    return total


def edge_pad(field, axis):
    size = field.shape[axis]
    low = lax.slice_in_dim(field, 0, 1, axis=axis)
    high = lax.slice_in_dim(field, size - 1, size, axis=axis)
    return jnp.concatenate([low, field, high], axis=axis)


def second(padded, axis):
    size = padded.shape[axis]
    upper = lax.slice_in_dim(padded, 2, size, axis=axis)
    lower = lax.slice_in_dim(padded, 0, size - 2, axis=axis)
    middle = lax.slice_in_dim(padded, 1, size - 1, axis=axis)
    return upper + lower - 2.0 * middle


def shift_space(block, forward):
    count = lax.axis_size("space")
    pairs = [(i, i + 1) for i in range(count - 1)]
    if not forward:
        pairs = [(t, s) for s, t in pairs]
    return lax.ppermute(block, "space", pairs)


def laplacian(volts, low, high, conduct):
    padded = jnp.concatenate([low, volts, high], axis=-3)
    lap = conduct[0] * second(padded, volts.ndim - 3)
    lap = lap + conduct[1] * second(edge_pad(volts, volts.ndim - 2), volts.ndim - 2)
    lap = lap + conduct[2] * second(edge_pad(volts, volts.ndim - 1), volts.ndim - 1)
    return lap


def close_edges(volts, depth, at_low, at_high):
    size = volts.shape[-3]
    inner_low = volts[..., depth : depth + 1, :, :]
    inner_high = volts[..., size - depth - 1 : size - depth, :, :]
    outer_low = jnp.where(at_low, inner_low, volts[..., depth - 1 : depth, :, :])
    outer_high = jnp.where(at_high, inner_high, volts[..., size - depth : size - depth + 1, :, :])
    return jnp.concatenate(
        [volts[..., : depth - 1, :, :], outer_low, volts[..., depth : size - depth, :, :], outer_high,
         volts[..., size - depth + 1 :, :, :]],
        axis=-3,
    )


def padded_laplacian(volts, conduct):
    x = volts.ndim - 3
    inner = lax.slice_in_dim(volts, 1, volts.shape[x] - 1, axis=x)
    lap = conduct[0] * second(volts, x)
    lap = lap + conduct[1] * second(edge_pad(inner, x + 1), x + 1)
    lap = lap + conduct[2] * second(edge_pad(inner, x + 2), x + 2)
    return lap


def coefficients(fibre, labels):
    fast_g = lookup(labels, [4.0, 3.0, 3.5, 1.0])
    slow_g = lookup(labels, [0.6, 0.9, 0.75, 0.3])
    slow_tau = 4.0 * lookup(labels, [1.0, 1.5, 1.2, 3.0])
    conduct = [0.2 + 0.6 * (fibre == d).astype(jnp.float32) for d in range(3)]
    return [fast_g, slow_g, slow_tau], conduct


def rates(states, lap, fast_g, slow_g, slow_tau):
    volt = states[..., 0, :, :, :]
    act = states[..., 1, :, :, :]
    inact = states[..., 2, :, :, :]
    slow = states[..., 3, :, :, :]
    current = (
        fast_g * act * act * act * inact * (volt - 1.0)
        + slow_g * slow * (volt + 0.2)
        + 0.3 * (volt + 0.1)
    )
    dvolt = lap - current
    dact = (jax.nn.sigmoid(8.0 * (volt - 0.2)) - act) / 0.5
    dinact = (jax.nn.sigmoid(-8.0 * (volt - 0.3)) - inact) / (
        1.0 + 3.0 * jax.nn.sigmoid(6.0 * (volt - 0.3))
    )
    dslow = (jax.nn.sigmoid(5.0 * (volt - 0.5)) - slow) / slow_tau
    return jnp.stack([dvolt, dact, dinact, dslow], axis=-4)


def quadrature(start, derivs, row):
    total = row[0] * derivs[0]
    for j in range(1, 5):
        total = total + row[j] * derivs[j]
    return start + slice_len * total


def edge_nodes(start, derivs, weights):
    total = weights[:, 0] * derivs[0][None]
    for j in range(1, 5):
        total = total + weights[:, j] * derivs[j][None]
    return start[None] + slice_len * total


def steps(guess, fibre, labels):
    table = radau_table()
    sums = [sum(row) for row in table]
    place = lax.axis_index("space")
    at_low = place == 0
    at_high = place == lax.axis_size("space") - 1
    first_slice = lax.axis_index("tm") == 0
    count = lax.axis_size("tm")
    tm_pairs = [(i, i + 1) for i in range(count - 1)]

    start0 = guess[0]
    volts0 = start0[0]
    planes = volts0.shape[0]

    code = (labels + 4 * fibre).astype(jnp.float32)
    top = jnp.concatenate([volts0[planes - 2 :], start0[1:, planes - 1], code[planes - 1 :]])
    bottom = jnp.concatenate([volts0[:2], start0[1:, 0], code[:1]])
    below = shift_space(top, True)
    above = shift_space(bottom, False)
    coef, conduct = coefficients(fibre, labels)
    edge_code = jnp.concatenate([below[5:6], above[5:6]]).astype(jnp.int32)
    edge_coef, edge_conduct = coefficients(edge_code // 4, edge_code % 4)
    widen = lambda core, edge: jnp.concatenate([edge[:1], core, edge[1:]])
    coef_ext = [widen(c, e) for c, e in zip(coef, edge_coef)]
    conduct_ext = [widen(c, e) for c, e in zip(conduct, edge_conduct)]
    fast_g, slow_g, slow_tau = coef

    volts_ext = jnp.concatenate([below[:2], volts0, above[:2]])
    gates_ext = jnp.concatenate([below[2:5][:, None], start0[1:], above[2:5][:, None]], axis=1)
    state_ext = jnp.concatenate([volts_ext[None, 1 : planes + 3], gates_ext])
    lap0 = padded_laplacian(close_edges(volts_ext, 2, at_low, at_high), conduct_ext)
    derivs0 = rates(state_ext, lap0, *coef_ext)
    ends0 = start0 + slice_len * (sums[4] * derivs0[:, 1 : planes + 1])
    arrived1 = lax.ppermute(ends0, "tm", tm_pairs)

    state_ext, derivs0, ends0 = lax.optimization_barrier((state_ext, derivs0, ends0))
    nodes0_ext = jnp.stack([state_ext + slice_len * (sums[m] * derivs0) for m in range(5)])
    nodes0 = nodes0_ext[:, :, 1 : planes + 1]
    lap1 = padded_laplacian(close_edges(nodes0_ext[:, 0], 1, at_low, at_high), conduct)
    derivs1 = rates(nodes0, lap1, fast_g, slow_g, slow_tau)
    start1 = jnp.where(first_slice, start0, arrived1)
    ends1 = quadrature(start1, derivs1, table[4])
    arrived2 = lax.ppermute(ends1, "tm", tm_pairs)
    weights = jnp.array(table, jnp.float32)[:, :, None, None, None]
    top = edge_nodes(start1[0, planes - 1 :], derivs1[:, 0, planes - 1 :], weights)
    bottom = edge_nodes(start1[0, :1], derivs1[:, 0, :1], weights)
    low2 = shift_space(top, True)
    high2 = shift_space(bottom, False)
    later_start, later_derivs, ends1 = lax.optimization_barrier((start1, derivs1, ends1))
    nodes1 = jnp.stack([quadrature(later_start, later_derivs, table[m]) for m in range(4)] + [ends1])

    volts2 = nodes1[:, 0]
    low2 = jnp.where(at_low, volts2[:, :1], low2)
    high2 = jnp.where(at_high, volts2[:, planes - 1 :], high2)
    derivs2 = rates(nodes1, laplacian(volts2, low2, high2, conduct), fast_g, slow_g, slow_tau)
    start2 = jnp.where(first_slice, start0, arrived2)
    ends2 = quadrature(start2, derivs2, table[4])
    return ends2[None]


def solution(mesh):
    placed = (P("tm", None, "space", None, None), P("space", None, None), P("space", None, None))
    return jax.shard_map(
        steps,
        mesh=mesh,
        in_specs=placed,
        out_specs=P("tm", None, "space", None, None),
        check_vma=False,
    )
```

```python
import jax
import jax.numpy as jnp
from jax import lax
from jax.sharding import PartitionSpec as P


radau_nodes = [0.05710419611451768, 0.2768430136381238, 0.5835904323689168, 0.8602401356562195, 1.0]
slice_len = 0.6


def radau_table():
    table = []
    for m in range(5):
        row_values = []
        for j in range(5):
            polynom = [1.0]
            for i in range(5):
                if i != j:
                    factor = radau_nodes[j] - radau_nodes[i]
                    shifted = [0.0] + [value / factor for value in polynom]
                    scaled = [-radau_nodes[i] * value / factor for value in polynom] + [0.0]
                    polynom = [shifted[p] + scaled[p] for p in range(len(polynom) + 1)]
            integral = 0.0
            for p in range(len(polynom)):
                integral = integral + polynom[p] * radau_nodes[m] ** (p + 1) / (p + 1)
            row_values.append(integral)
        table.append(row_values)
    return table


def lookup(labels, values):
    total = jnp.zeros(labels.shape, jnp.float32)
    for level in range(len(values)):
        total = total + jnp.where(labels == level, values[level], 0.0).astype(jnp.float32)
    return total


def edge_pad(field, axis):
    size = field.shape[axis]
    low = lax.slice_in_dim(field, 0, 1, axis=axis)
    high = lax.slice_in_dim(field, size - 1, size, axis=axis)
    return jnp.concatenate([low, field, high], axis=axis)


def second(padded, axis):
    size = padded.shape[axis]
    upper = lax.slice_in_dim(padded, 2, size, axis=axis)
    lower = lax.slice_in_dim(padded, 0, size - 2, axis=axis)
    middle = lax.slice_in_dim(padded, 1, size - 1, axis=axis)
    return upper + lower - 2.0 * middle


def shift_space(block, forward):
    count = lax.axis_size("space")
    pairs = [(i, i + 1) for i in range(count - 1)]
    if not forward:
        pairs = [(t, s) for s, t in pairs]
    return lax.ppermute(block, "space", pairs)


def close_edges(volts, depth, at_low, at_high):
    size = volts.shape[-3]
    inner_low = volts[..., depth : depth + 1, :, :]
    inner_high = volts[..., size - depth - 1 : size - depth, :, :]
    outer_low = jnp.where(at_low, inner_low, volts[..., depth - 1 : depth, :, :])
    outer_high = jnp.where(at_high, inner_high, volts[..., size - depth : size - depth + 1, :, :])
    return jnp.concatenate(
        [volts[..., : depth - 1, :, :], outer_low, volts[..., depth : size - depth, :, :], outer_high,
         volts[..., size - depth + 1 :, :, :]],
        axis=-3,
    )


def padded_laplacian(volts, conduct):
    x = volts.ndim - 3
    inner = lax.slice_in_dim(volts, 1, volts.shape[x] - 1, axis=x)
    lap = conduct[0] * second(volts, x)
    lap = lap + conduct[1] * second(edge_pad(inner, x + 1), x + 1)
    lap = lap + conduct[2] * second(edge_pad(inner, x + 2), x + 2)
    return lap


def coefficients(fibre, labels):
    fast_g = lookup(labels, [4.0, 3.0, 3.5, 1.0])
    slow_g = lookup(labels, [0.6, 0.9, 0.75, 0.3])
    slow_tau = 4.0 * lookup(labels, [1.0, 1.5, 1.2, 3.0])
    conduct = [0.2 + 0.6 * (fibre == d).astype(jnp.float32) for d in range(3)]
    return [fast_g, slow_g, slow_tau], conduct


def rates(states, lap, fast_g, slow_g, slow_tau):
    volt = states[..., 0, :, :, :]
    act = states[..., 1, :, :, :]
    inact = states[..., 2, :, :, :]
    slow = states[..., 3, :, :, :]
    current = (
        fast_g * act * act * act * inact * (volt - 1.0)
        + slow_g * slow * (volt + 0.2)
        + 0.3 * (volt + 0.1)
    )
    dvolt = lap - current
    dact = (jax.nn.sigmoid(8.0 * (volt - 0.2)) - act) / 0.5
    dinact = (jax.nn.sigmoid(-8.0 * (volt - 0.3)) - inact) / (
        1.0 + 3.0 * jax.nn.sigmoid(6.0 * (volt - 0.3))
    )
    dslow = (jax.nn.sigmoid(5.0 * (volt - 0.5)) - slow) / slow_tau
    return jnp.stack([dvolt, dact, dinact, dslow], axis=-4)


def quadrature(start, derivs, row):
    total = row[0] * derivs[0]
    for j in range(1, 5):
        total = total + row[j] * derivs[j]
    return start + slice_len * total


def steps(guess, fibre, labels):
    table = radau_table()
    sums = [sum(row) for row in table]
    place = lax.axis_index("space")
    at_low = place == 0
    at_high = place == lax.axis_size("space") - 1
    first_slice = lax.axis_index("tm") == 0
    count = lax.axis_size("tm")
    tm_pairs = [(i, i + 1) for i in range(count - 1)]

    start0 = guess[0]
    volts0 = start0[0]
    planes = volts0.shape[0]
    rows = start0.shape[2:]

    code = (labels + 4 * fibre).astype(jnp.float32)
    top = jnp.concatenate([volts0[planes - 2 :], start0[1:, planes - 1], code[planes - 1 :]])
    bottom = jnp.concatenate([volts0[:2], start0[1:, 0], code[:1]])
    below = shift_space(top, True)
    above = shift_space(bottom, False)
    coef, conduct = coefficients(fibre, labels)
    edge_code = jnp.concatenate([below[5:6], above[5:6]]).astype(jnp.int32)
    edge_coef, edge_conduct = coefficients(edge_code // 4, edge_code % 4)
    widen = lambda core, edge: jnp.concatenate([edge[:1], core, edge[1:]])
    coef_ext = [widen(c, e) for c, e in zip(coef, edge_coef)]
    conduct_ext = [widen(c, e) for c, e in zip(conduct, edge_conduct)]
    fast_g, slow_g, slow_tau = coef

    volts_ext = jnp.concatenate([below[:2], volts0, above[:2]])
    gates_ext = jnp.concatenate([below[2:5][:, None], start0[1:], above[2:5][:, None]], axis=1)
    state_ext = jnp.concatenate([volts_ext[None, 1 : planes + 3], gates_ext])
    lap0 = padded_laplacian(close_edges(volts_ext, 2, at_low, at_high), conduct_ext)
    derivs0 = rates(state_ext, lap0, *coef_ext)
    ends0 = state_ext + slice_len * (sums[4] * derivs0)
    fields = start0.shape[0]
    message1 = jnp.concatenate(
        [ends0[:, 1 : planes + 1].reshape(fields * planes, *rows), ends0[0, :1], ends0[0, planes + 1 :]]
    )
    state_ext, derivs0, message1 = lax.optimization_barrier((state_ext, derivs0, message1))
    arrived1 = lax.ppermute(message1, "tm", tm_pairs)
    nodes0_ext = jnp.stack([state_ext + slice_len * (sums[m] * derivs0) for m in range(5)])
    nodes0 = nodes0_ext[:, :, 1 : planes + 1]
    lap1 = padded_laplacian(close_edges(nodes0_ext[:, 0], 1, at_low, at_high), conduct)
    derivs1 = rates(nodes0, lap1, fast_g, slow_g, slow_tau)
    low_f = shift_space(derivs1[:, 0, planes - 1 :], True)
    high_f = shift_space(derivs1[:, 0, :1], False)
    block1 = arrived1[: fields * planes].reshape(start0.shape)
    start1 = jnp.where(first_slice, start0, block1)
    start1_volts = jnp.where(
        first_slice,
        volts_ext[1 : planes + 3],
        jnp.concatenate([arrived1[fields * planes : fields * planes + 1], block1[0], arrived1[fields * planes + 1 :]]),
    )
    ends1 = quadrature(start1, derivs1, table[4])
    arrived2 = lax.ppermute(ends1, "tm", tm_pairs)
    later = lax.optimization_barrier((start1, start1_volts, derivs1, low_f, high_f, ends1))
    later_start, later_volts, later_derivs, low_f, high_f, ends1 = later
    dvolts1 = jnp.concatenate([low_f, later_derivs[:, 0], high_f], axis=1)
    volts1 = jnp.stack([quadrature(later_volts, dvolts1, table[m]) for m in range(5)])
    gates1 = jnp.stack([quadrature(later_start[1:], later_derivs[:, 1:], table[m]) for m in range(5)])
    nodes1 = jnp.concatenate([volts1[:, None, 1 : planes + 1], gates1], axis=1)

    lap2 = padded_laplacian(close_edges(volts1, 1, at_low, at_high), conduct)
    derivs2 = rates(nodes1, lap2, fast_g, slow_g, slow_tau)
    start2 = jnp.where(first_slice, start0, arrived2)
    ends2 = quadrature(start2, derivs2, table[4])
    return ends2[None]


def solution(mesh):
    placed = (P("tm", None, "space", None, None), P("space", None, None), P("space", None, None))
    return jax.shard_map(
        steps,
        mesh=mesh,
        in_specs=placed,
        out_specs=P("tm", None, "space", None, None),
        check_vma=False,
    )
```

```python
import jax
import jax.numpy as jnp
from jax import lax
from jax.sharding import PartitionSpec as P


radau_nodes = [0.05710419611451768, 0.2768430136381238, 0.5835904323689168, 0.8602401356562195, 1.0]
slice_len = 0.6


def radau_table():
    table = []
    for m in range(5):
        row_values = []
        for j in range(5):
            polynom = [1.0]
            for i in range(5):
                if i != j:
                    factor = radau_nodes[j] - radau_nodes[i]
                    shifted = [0.0] + [value / factor for value in polynom]
                    scaled = [-radau_nodes[i] * value / factor for value in polynom] + [0.0]
                    polynom = [shifted[p] + scaled[p] for p in range(len(polynom) + 1)]
            integral = 0.0
            for p in range(len(polynom)):
                integral = integral + polynom[p] * radau_nodes[m] ** (p + 1) / (p + 1)
            row_values.append(integral)
        table.append(row_values)
    return table


def lookup(labels, values):
    total = jnp.zeros(labels.shape, jnp.float32)
    for level in range(len(values)):
        total = total + jnp.where(labels == level, values[level], 0.0).astype(jnp.float32)
    return total


def edge_pad(field, axis):
    size = field.shape[axis]
    low = lax.slice_in_dim(field, 0, 1, axis=axis)
    high = lax.slice_in_dim(field, size - 1, size, axis=axis)
    return jnp.concatenate([low, field, high], axis=axis)


def second(padded, axis):
    size = padded.shape[axis]
    upper = lax.slice_in_dim(padded, 2, size, axis=axis)
    lower = lax.slice_in_dim(padded, 0, size - 2, axis=axis)
    middle = lax.slice_in_dim(padded, 1, size - 1, axis=axis)
    return upper + lower - 2.0 * middle


def shift_space(block, forward):
    count = lax.axis_size("space")
    pairs = [(i, i + 1) for i in range(count - 1)]
    if not forward:
        pairs = [(t, s) for s, t in pairs]
    return lax.ppermute(block, "space", pairs)


def halos(volts):
    planes = volts.shape[-3]
    low = shift_space(volts[..., planes - 1 : planes, :, :], True)
    high = shift_space(volts[..., 0:1, :, :], False)
    return low, high


def laplacian(volts, low, high, conduct):
    padded = jnp.concatenate([low, volts, high], axis=-3)
    lap = conduct[0] * second(padded, volts.ndim - 3)
    lap = lap + conduct[1] * second(edge_pad(volts, volts.ndim - 2), volts.ndim - 2)
    lap = lap + conduct[2] * second(edge_pad(volts, volts.ndim - 1), volts.ndim - 1)
    return lap


def rates(states, lap, fast_g, slow_g, slow_tau):
    volt = states[..., 0, :, :, :]
    act = states[..., 1, :, :, :]
    inact = states[..., 2, :, :, :]
    slow = states[..., 3, :, :, :]
    current = (
        fast_g * act * act * act * inact * (volt - 1.0)
        + slow_g * slow * (volt + 0.2)
        + 0.3 * (volt + 0.1)
    )
    dvolt = lap - current
    dact = (jax.nn.sigmoid(8.0 * (volt - 0.2)) - act) / 0.5
    dinact = (jax.nn.sigmoid(-8.0 * (volt - 0.3)) - inact) / (
        1.0 + 3.0 * jax.nn.sigmoid(6.0 * (volt - 0.3))
    )
    dslow = (jax.nn.sigmoid(5.0 * (volt - 0.5)) - slow) / slow_tau
    return jnp.stack([dvolt, dact, dinact, dslow], axis=-4)


def increment(derivs, row):
    total = row[0] * derivs[0]
    for j in range(1, 5):
        total = total + row[j] * derivs[j]
    return slice_len * total


def quadrature(start, derivs, row):
    return start + increment(derivs, row)


def steps(guess, fibre, labels):
    table = radau_table()
    sums = [sum(row) for row in table]
    fast_g = lookup(labels, [4.0, 3.0, 3.5, 1.0])
    slow_g = lookup(labels, [0.6, 0.9, 0.75, 0.3])
    slow_tau = 4.0 * lookup(labels, [1.0, 1.5, 1.2, 3.0])
    conduct = [0.2 + 0.6 * (fibre == d).astype(jnp.float32) for d in range(3)]
    place = lax.axis_index("space")
    at_low = place == 0
    at_high = place == lax.axis_size("space") - 1
    first_slice = lax.axis_index("tm") == 0
    count = lax.axis_size("tm")
    tm_pairs = [(i, i + 1) for i in range(count - 1)]

    start0 = guess[0]
    volts0 = start0[0]
    planes = volts0.shape[0]

    low0, high0 = halos(volts0)
    low0 = jnp.where(at_low, volts0[:1], low0)
    high0 = jnp.where(at_high, volts0[planes - 1 :], high0)
    derivs0 = rates(start0, laplacian(volts0, low0, high0, conduct), fast_g, slow_g, slow_tau)
    ends0 = start0 + slice_len * (sums[4] * derivs0)
    arrived1 = lax.ppermute(ends0, "tm", tm_pairs)

    dv = derivs0[0]
    dlow, dhigh = halos(dv)
    nodes0 = jnp.stack([start0 + slice_len * (sums[m] * derivs0) for m in range(5)])
    volts1 = nodes0[:, 0]
    low1 = jnp.stack([low0 + slice_len * (sums[m] * dlow) for m in range(5)])
    high1 = jnp.stack([high0 + slice_len * (sums[m] * dhigh) for m in range(5)])
    low1 = jnp.where(at_low, volts1[:, :1], low1)
    high1 = jnp.where(at_high, volts1[:, planes - 1 :], high1)
    derivs1 = rates(nodes0, laplacian(volts1, low1, high1, conduct), fast_g, slow_g, slow_tau)
    step1 = lax.optimization_barrier(increment(derivs1, table[4]))
    start1 = jnp.where(first_slice, start0, arrived1)
    ends1 = start1 + step1
    arrived2 = lax.ppermute(ends1, "tm", tm_pairs)
    later_start, later_derivs, ends1 = lax.optimization_barrier((start1, derivs1, ends1))
    nodes1 = jnp.stack([quadrature(later_start, later_derivs, table[m]) for m in range(4)] + [ends1])

    volts2 = nodes1[:, 0]
    low2, high2 = halos(volts2)
    low2 = jnp.where(at_low, volts2[:, :1], low2)
    high2 = jnp.where(at_high, volts2[:, planes - 1 :], high2)
    derivs2 = rates(nodes1, laplacian(volts2, low2, high2, conduct), fast_g, slow_g, slow_tau)
    step2 = lax.optimization_barrier(increment(derivs2, table[4]))
    start2 = jnp.where(first_slice, start0, arrived2)
    ends2 = start2 + step2
    return ends2[None]


def solution(mesh):
    placed = (P("tm", None, "space", None, None), P("space", None, None), P("space", None, None))
    return jax.shard_map(
        steps,
        mesh=mesh,
        in_specs=placed,
        out_specs=P("tm", None, "space", None, None),
        check_vma=False,
    )
```

```python
import jax
import jax.numpy as jnp
from jax import lax
from jax.sharding import PartitionSpec as P


radau_nodes = [0.05710419611451768, 0.2768430136381238, 0.5835904323689168, 0.8602401356562195, 1.0]
slice_len = 0.6


def radau_table():
    table = []
    for m in range(5):
        row_values = []
        for j in range(5):
            polynom = [1.0]
            for i in range(5):
                if i != j:
                    factor = radau_nodes[j] - radau_nodes[i]
                    shifted = [0.0] + [value / factor for value in polynom]
                    scaled = [-radau_nodes[i] * value / factor for value in polynom] + [0.0]
                    polynom = [shifted[p] + scaled[p] for p in range(len(polynom) + 1)]
            integral = 0.0
            for p in range(len(polynom)):
                integral = integral + polynom[p] * radau_nodes[m] ** (p + 1) / (p + 1)
            row_values.append(integral)
        table.append(row_values)
    return table


def lookup(labels, values):
    total = jnp.zeros(labels.shape, jnp.float32)
    for level in range(len(values)):
        total = total + jnp.where(labels == level, values[level], 0.0).astype(jnp.float32)
    return total


def edge_pad(field, axis):
    size = field.shape[axis]
    low = lax.slice_in_dim(field, 0, 1, axis=axis)
    high = lax.slice_in_dim(field, size - 1, size, axis=axis)
    return jnp.concatenate([low, field, high], axis=axis)


def second(padded, axis):
    size = padded.shape[axis]
    upper = lax.slice_in_dim(padded, 2, size, axis=axis)
    lower = lax.slice_in_dim(padded, 0, size - 2, axis=axis)
    middle = lax.slice_in_dim(padded, 1, size - 1, axis=axis)
    return upper + lower - 2.0 * middle


def shift_space(block, forward):
    count = lax.axis_size("space")
    pairs = [(i, i + 1) for i in range(count - 1)]
    if not forward:
        pairs = [(t, s) for s, t in pairs]
    return lax.ppermute(block, "space", pairs)


def halos(volts):
    planes = volts.shape[-3]
    low = shift_space(volts[..., planes - 1 : planes, :, :], True)
    high = shift_space(volts[..., 0:1, :, :], False)
    return low, high


def laplacian(volts, low, high, conduct):
    padded = jnp.concatenate([low, volts, high], axis=-3)
    lap = conduct[0] * second(padded, volts.ndim - 3)
    lap = lap + conduct[1] * second(edge_pad(volts, volts.ndim - 2), volts.ndim - 2)
    lap = lap + conduct[2] * second(edge_pad(volts, volts.ndim - 1), volts.ndim - 1)
    return lap


def rates(states, lap, fast_g, slow_g, slow_tau):
    volt = states[..., 0, :, :, :]
    act = states[..., 1, :, :, :]
    inact = states[..., 2, :, :, :]
    slow = states[..., 3, :, :, :]
    current = (
        fast_g * act * act * act * inact * (volt - 1.0)
        + slow_g * slow * (volt + 0.2)
        + 0.3 * (volt + 0.1)
    )
    dvolt = lap - current
    dact = (jax.nn.sigmoid(8.0 * (volt - 0.2)) - act) / 0.5
    dinact = (jax.nn.sigmoid(-8.0 * (volt - 0.3)) - inact) / (
        1.0 + 3.0 * jax.nn.sigmoid(6.0 * (volt - 0.3))
    )
    dslow = (jax.nn.sigmoid(5.0 * (volt - 0.5)) - slow) / slow_tau
    return jnp.stack([dvolt, dact, dinact, dslow], axis=-4)


def increment(derivs, row):
    total = row[0] * derivs[0]
    for j in range(1, 5):
        total = total + row[j] * derivs[j]
    return slice_len * total


def quadrature(start, derivs, row):
    return start + increment(derivs, row)


def edge_nodes(start, derivs, weights):
    total = weights[:, 0] * derivs[0][None]
    for j in range(1, 5):
        total = total + weights[:, j] * derivs[j][None]
    return start[None] + slice_len * total


def steps(guess, fibre, labels):
    table = radau_table()
    sums = [sum(row) for row in table]
    fast_g = lookup(labels, [4.0, 3.0, 3.5, 1.0])
    slow_g = lookup(labels, [0.6, 0.9, 0.75, 0.3])
    slow_tau = 4.0 * lookup(labels, [1.0, 1.5, 1.2, 3.0])
    conduct = [0.2 + 0.6 * (fibre == d).astype(jnp.float32) for d in range(3)]
    place = lax.axis_index("space")
    at_low = place == 0
    at_high = place == lax.axis_size("space") - 1
    first_slice = lax.axis_index("tm") == 0
    count = lax.axis_size("tm")
    tm_pairs = [(i, i + 1) for i in range(count - 1)]

    start0 = guess[0]
    volts0 = start0[0]
    planes = volts0.shape[0]

    low0, high0 = halos(volts0)
    low0 = jnp.where(at_low, volts0[:1], low0)
    high0 = jnp.where(at_high, volts0[planes - 1 :], high0)
    derivs0 = rates(start0, laplacian(volts0, low0, high0, conduct), fast_g, slow_g, slow_tau)
    ends0 = start0 + slice_len * (sums[4] * derivs0)
    arrived1 = lax.ppermute(ends0, "tm", tm_pairs)

    dv = derivs0[0]
    dlow, dhigh = halos(dv)
    nodes0 = jnp.stack([start0 + slice_len * (sums[m] * derivs0) for m in range(5)])
    volts1 = nodes0[:, 0]
    low1 = jnp.stack([low0 + slice_len * (sums[m] * dlow) for m in range(5)])
    high1 = jnp.stack([high0 + slice_len * (sums[m] * dhigh) for m in range(5)])
    low1 = jnp.where(at_low, volts1[:, :1], low1)
    high1 = jnp.where(at_high, volts1[:, planes - 1 :], high1)
    derivs1 = rates(nodes0, laplacian(volts1, low1, high1, conduct), fast_g, slow_g, slow_tau)
    step1 = lax.optimization_barrier(increment(derivs1, table[4]))
    start1 = jnp.where(first_slice, start0, arrived1)
    ends1 = start1 + step1
    arrived2 = lax.ppermute(ends1, "tm", tm_pairs)
    later_start, later_derivs, ends1 = lax.optimization_barrier((start1, derivs1, ends1))
    weights = jnp.array(table, jnp.float32)[:, :, None, None, None]
    top = edge_nodes(later_start[0, planes - 1 :], later_derivs[:, 0, planes - 1 :], weights)
    bottom = edge_nodes(later_start[0, :1], later_derivs[:, 0, :1], weights)
    low2 = shift_space(top, True)
    high2 = shift_space(bottom, False)
    nodes1 = jnp.stack([quadrature(later_start, later_derivs, table[m]) for m in range(4)] + [ends1])

    volts2 = nodes1[:, 0]
    low2 = jnp.where(at_low, volts2[:, :1], low2)
    high2 = jnp.where(at_high, volts2[:, planes - 1 :], high2)
    derivs2 = rates(nodes1, laplacian(volts2, low2, high2, conduct), fast_g, slow_g, slow_tau)
    step2 = lax.optimization_barrier(increment(derivs2, table[4]))
    start2 = jnp.where(first_slice, start0, arrived2)
    ends2 = start2 + step2
    return ends2[None]


def solution(mesh):
    placed = (P("tm", None, "space", None, None), P("space", None, None), P("space", None, None))
    return jax.shard_map(
        steps,
        mesh=mesh,
        in_specs=placed,
        out_specs=P("tm", None, "space", None, None),
        check_vma=False,
    )
```

```python
import jax
import jax.numpy as jnp
from jax import lax
from jax.sharding import PartitionSpec as P


radau_nodes = [0.05710419611451768, 0.2768430136381238, 0.5835904323689168, 0.8602401356562195, 1.0]
slice_len = 0.6


def radau_table():
    table = []
    for m in range(5):
        row_values = []
        for j in range(5):
            polynom = [1.0]
            for i in range(5):
                if i != j:
                    factor = radau_nodes[j] - radau_nodes[i]
                    shifted = [0.0] + [value / factor for value in polynom]
                    scaled = [-radau_nodes[i] * value / factor for value in polynom] + [0.0]
                    polynom = [shifted[p] + scaled[p] for p in range(len(polynom) + 1)]
            integral = 0.0
            for p in range(len(polynom)):
                integral = integral + polynom[p] * radau_nodes[m] ** (p + 1) / (p + 1)
            row_values.append(integral)
        table.append(row_values)
    return table


def lookup(labels, values):
    total = jnp.zeros(labels.shape, jnp.float32)
    for level in range(len(values)):
        total = total + jnp.where(labels == level, values[level], 0.0).astype(jnp.float32)
    return total


def edge_pad(field, axis):
    size = field.shape[axis]
    low = lax.slice_in_dim(field, 0, 1, axis=axis)
    high = lax.slice_in_dim(field, size - 1, size, axis=axis)
    return jnp.concatenate([low, field, high], axis=axis)


def second(padded, axis):
    size = padded.shape[axis]
    upper = lax.slice_in_dim(padded, 2, size, axis=axis)
    lower = lax.slice_in_dim(padded, 0, size - 2, axis=axis)
    middle = lax.slice_in_dim(padded, 1, size - 1, axis=axis)
    return upper + lower - 2.0 * middle


def shift_space(block, forward):
    count = lax.axis_size("space")
    pairs = [(i, i + 1) for i in range(count - 1)]
    if not forward:
        pairs = [(t, s) for s, t in pairs]
    return lax.ppermute(block, "space", pairs)


def halos(volts):
    planes = volts.shape[-3]
    low = shift_space(volts[..., planes - 1 : planes, :, :], True)
    high = shift_space(volts[..., 0:1, :, :], False)
    return low, high


def laplacian(volts, low, high, conduct):
    padded = jnp.concatenate([low, volts, high], axis=-3)
    lap = conduct[0] * second(padded, volts.ndim - 3)
    lap = lap + conduct[1] * second(edge_pad(volts, volts.ndim - 2), volts.ndim - 2)
    lap = lap + conduct[2] * second(edge_pad(volts, volts.ndim - 1), volts.ndim - 1)
    return lap


def rates(states, lap, fast_g, slow_g, slow_tau):
    volt = states[..., 0, :, :, :]
    act = states[..., 1, :, :, :]
    inact = states[..., 2, :, :, :]
    slow = states[..., 3, :, :, :]
    current = (
        fast_g * act * act * act * inact * (volt - 1.0)
        + slow_g * slow * (volt + 0.2)
        + 0.3 * (volt + 0.1)
    )
    dvolt = lap - current
    dact = (jax.nn.sigmoid(8.0 * (volt - 0.2)) - act) / 0.5
    dinact = (jax.nn.sigmoid(-8.0 * (volt - 0.3)) - inact) / (
        1.0 + 3.0 * jax.nn.sigmoid(6.0 * (volt - 0.3))
    )
    dslow = (jax.nn.sigmoid(5.0 * (volt - 0.5)) - slow) / slow_tau
    return jnp.stack([dvolt, dact, dinact, dslow], axis=-4)


def increment(derivs, row):
    total = row[0] * derivs[0]
    for j in range(1, 5):
        total = total + row[j] * derivs[j]
    return slice_len * total


def edge_nodes(start, derivs, weights):
    total = weights[:, 0] * derivs[0][None]
    for j in range(1, 5):
        total = total + weights[:, j] * derivs[j][None]
    return start[None] + slice_len * total


def steps(guess, fibre, labels):
    table = radau_table()
    sums = [sum(row) for row in table]
    fast_g = lookup(labels, [4.0, 3.0, 3.5, 1.0])
    slow_g = lookup(labels, [0.6, 0.9, 0.75, 0.3])
    slow_tau = 4.0 * lookup(labels, [1.0, 1.5, 1.2, 3.0])
    conduct = [0.2 + 0.6 * (fibre == d).astype(jnp.float32) for d in range(3)]
    place = lax.axis_index("space")
    at_low = place == 0
    at_high = place == lax.axis_size("space") - 1
    first_slice = lax.axis_index("tm") == 0
    count = lax.axis_size("tm")
    tm_pairs = [(i, i + 1) for i in range(count - 1)]

    start0 = guess[0]
    volts0 = start0[0]
    planes = volts0.shape[0]

    low0, high0 = halos(volts0)
    low0 = jnp.where(at_low, volts0[:1], low0)
    high0 = jnp.where(at_high, volts0[planes - 1 :], high0)
    derivs0 = rates(start0, laplacian(volts0, low0, high0, conduct), fast_g, slow_g, slow_tau)
    ends0 = start0 + slice_len * (sums[4] * derivs0)
    derivs0, ends0 = lax.optimization_barrier((derivs0, ends0))
    arrived1 = lax.ppermute(ends0, "tm", tm_pairs)

    dv = derivs0[0]
    dlow, dhigh = halos(dv)
    nodes0 = jnp.stack([start0 + slice_len * (sums[m] * derivs0) for m in range(5)])
    volts1 = nodes0[:, 0]
    low1 = jnp.stack([low0 + slice_len * (sums[m] * dlow) for m in range(5)])
    high1 = jnp.stack([high0 + slice_len * (sums[m] * dhigh) for m in range(5)])
    low1 = jnp.where(at_low, volts1[:, :1], low1)
    high1 = jnp.where(at_high, volts1[:, planes - 1 :], high1)
    derivs1 = rates(nodes0, laplacian(volts1, low1, high1, conduct), fast_g, slow_g, slow_tau)
    step1 = lax.optimization_barrier(increment(derivs1, table[4]))
    start1 = jnp.where(first_slice, start0, arrived1)
    ends1 = start1 + step1
    arrived2 = lax.ppermute(ends1, "tm", tm_pairs)
    later_start, later_derivs, ends1 = lax.optimization_barrier((start1, derivs1, ends1))
    weights = jnp.array(table, jnp.float32)[:, :, None, None, None]
    top = edge_nodes(later_start[0, planes - 1 :], later_derivs[:, 0, planes - 1 :], weights)
    bottom = edge_nodes(later_start[0, :1], later_derivs[:, 0, :1], weights)
    low2 = shift_space(top, True)
    high2 = shift_space(bottom, False)
    nodes1 = edge_nodes(later_start, later_derivs, weights[..., None])

    volts2 = nodes1[:, 0]
    low2 = jnp.where(at_low, volts2[:, :1], low2)
    high2 = jnp.where(at_high, volts2[:, planes - 1 :], high2)
    derivs2 = rates(nodes1, laplacian(volts2, low2, high2, conduct), fast_g, slow_g, slow_tau)
    step2 = lax.optimization_barrier(increment(derivs2, table[4]))
    start2 = jnp.where(first_slice, start0, arrived2)
    ends2 = start2 + step2
    return ends2[None]


def solution(mesh):
    placed = (P("tm", None, "space", None, None), P("space", None, None), P("space", None, None))
    return jax.shard_map(
        steps,
        mesh=mesh,
        in_specs=placed,
        out_specs=P("tm", None, "space", None, None),
        check_vma=False,
    )
```

```python
import jax
import jax.numpy as jnp
from jax import lax
from jax.sharding import PartitionSpec as P


radau_nodes = [0.05710419611451768, 0.2768430136381238, 0.5835904323689168, 0.8602401356562195, 1.0]
slice_len = 0.6


def radau_table():
    table = []
    for m in range(5):
        row_values = []
        for j in range(5):
            polynom = [1.0]
            for i in range(5):
                if i != j:
                    factor = radau_nodes[j] - radau_nodes[i]
                    shifted = [0.0] + [value / factor for value in polynom]
                    scaled = [-radau_nodes[i] * value / factor for value in polynom] + [0.0]
                    polynom = [shifted[p] + scaled[p] for p in range(len(polynom) + 1)]
            integral = 0.0
            for p in range(len(polynom)):
                integral = integral + polynom[p] * radau_nodes[m] ** (p + 1) / (p + 1)
            row_values.append(integral)
        table.append(row_values)
    return table


def lookup(labels, values):
    total = jnp.zeros(labels.shape, jnp.float32)
    for level in range(len(values)):
        total = total + jnp.where(labels == level, values[level], 0.0).astype(jnp.float32)
    return total


def edge_pad(field, axis):
    size = field.shape[axis]
    low = lax.slice_in_dim(field, 0, 1, axis=axis)
    high = lax.slice_in_dim(field, size - 1, size, axis=axis)
    return jnp.concatenate([low, field, high], axis=axis)


def second(padded, axis):
    size = padded.shape[axis]
    upper = lax.slice_in_dim(padded, 2, size, axis=axis)
    lower = lax.slice_in_dim(padded, 0, size - 2, axis=axis)
    middle = lax.slice_in_dim(padded, 1, size - 1, axis=axis)
    return upper + lower - 2.0 * middle


def shift_space(block, forward):
    count = lax.axis_size("space")
    pairs = [(i, i + 1) for i in range(count - 1)]
    if not forward:
        pairs = [(t, s) for s, t in pairs]
    return lax.ppermute(block, "space", pairs)


def halos(volts):
    planes = volts.shape[-3]
    low = shift_space(volts[..., planes - 1 : planes, :, :], True)
    high = shift_space(volts[..., 0:1, :, :], False)
    return low, high


def laplacian(volts, low, high, conduct):
    padded = jnp.concatenate([low, volts, high], axis=-3)
    lap = conduct[0] * second(padded, volts.ndim - 3)
    lap = lap + conduct[1] * second(edge_pad(volts, volts.ndim - 2), volts.ndim - 2)
    lap = lap + conduct[2] * second(edge_pad(volts, volts.ndim - 1), volts.ndim - 1)
    return lap


def rates(states, lap, fast_g, slow_g, slow_tau):
    volt = states[..., 0, :, :, :]
    act = states[..., 1, :, :, :]
    inact = states[..., 2, :, :, :]
    slow = states[..., 3, :, :, :]
    current = (
        fast_g * act * act * act * inact * (volt - 1.0)
        + slow_g * slow * (volt + 0.2)
        + 0.3 * (volt + 0.1)
    )
    dvolt = lap - current
    dact = (jax.nn.sigmoid(8.0 * (volt - 0.2)) - act) / 0.5
    dinact = (jax.nn.sigmoid(-8.0 * (volt - 0.3)) - inact) / (
        1.0 + 3.0 * jax.nn.sigmoid(6.0 * (volt - 0.3))
    )
    dslow = (jax.nn.sigmoid(5.0 * (volt - 0.5)) - slow) / slow_tau
    return jnp.stack([dvolt, dact, dinact, dslow], axis=-4)


def increment(derivs, row):
    total = row[0] * derivs[0]
    for j in range(1, 5):
        total = total + row[j] * derivs[j]
    return slice_len * total


def edge_nodes(start, derivs, weights):
    total = weights[:, 0] * derivs[0][None]
    for j in range(1, 5):
        total = total + weights[:, j] * derivs[j][None]
    return start[None] + slice_len * total


def steps(guess, fibre, labels):
    table = radau_table()
    sums = [sum(row) for row in table]
    fast_g = lookup(labels, [4.0, 3.0, 3.5, 1.0])
    slow_g = lookup(labels, [0.6, 0.9, 0.75, 0.3])
    slow_tau = 4.0 * lookup(labels, [1.0, 1.5, 1.2, 3.0])
    conduct = [0.2 + 0.6 * (fibre == d).astype(jnp.float32) for d in range(3)]
    place = lax.axis_index("space")
    at_low = place == 0
    at_high = place == lax.axis_size("space") - 1
    first_slice = lax.axis_index("tm") == 0
    count = lax.axis_size("tm")
    tm_pairs = [(i, i + 1) for i in range(count - 1)]

    start0 = guess[0]
    volts0 = start0[0]
    planes = volts0.shape[0]

    low0, high0 = halos(volts0)
    low0 = jnp.where(at_low, volts0[:1], low0)
    high0 = jnp.where(at_high, volts0[planes - 1 :], high0)
    derivs0 = rates(start0, laplacian(volts0, low0, high0, conduct), fast_g, slow_g, slow_tau)
    ends0 = start0 + slice_len * (sums[4] * derivs0)
    derivs0, ends0 = lax.optimization_barrier((derivs0, ends0))
    arrived1 = lax.ppermute(ends0, "tm", tm_pairs)

    dv = derivs0[0]
    dlow, dhigh = halos(dv)
    nodes0 = jnp.stack([start0 + slice_len * (sums[m] * derivs0) for m in range(5)])
    volts1 = nodes0[:, 0]
    low1 = jnp.stack([low0 + slice_len * (sums[m] * dlow) for m in range(5)])
    high1 = jnp.stack([high0 + slice_len * (sums[m] * dhigh) for m in range(5)])
    low1 = jnp.where(at_low, volts1[:, :1], low1)
    high1 = jnp.where(at_high, volts1[:, planes - 1 :], high1)
    derivs1 = rates(nodes0, laplacian(volts1, low1, high1, conduct), fast_g, slow_g, slow_tau)
    step1 = lax.optimization_barrier(increment(derivs1, table[4]))
    start1 = jnp.where(first_slice, start0, arrived1)
    ends1 = start1 + step1
    arrived2 = lax.ppermute(ends1, "tm", tm_pairs)
    later_start, later_derivs, ends1 = lax.optimization_barrier((start1, derivs1, ends1))
    weights = jnp.array(table, jnp.float32)[:, :, None, None, None]
    top = edge_nodes(later_start[0, planes - 1 :], later_derivs[:, 0, planes - 1 :], weights)
    bottom = edge_nodes(later_start[0, :1], later_derivs[:, 0, :1], weights)
    low2 = shift_space(top, True)
    high2 = shift_space(bottom, False)
    nodes1 = edge_nodes(later_start, later_derivs, weights[..., None])

    volts2 = nodes1[:, 0]
    low2 = jnp.where(at_low, volts2[:, :1], low2)
    high2 = jnp.where(at_high, volts2[:, planes - 1 :], high2)
    rough = rates(nodes1, laplacian(volts2, volts2[:, :1], volts2[:, planes - 1 :], conduct), fast_g, slow_g, slow_tau)
    step2 = lax.optimization_barrier(increment(rough, table[4]))

    def edge_plane(lo, hi, below, above):
        part = lambda c: c[lo:hi]
        lap = laplacian(volts2[:, lo:hi], below, above, [part(c) for c in conduct])
        derivs = rates(nodes1[:, :, lo:hi], lap, part(fast_g), part(slow_g), part(slow_tau))
        return increment(derivs, table[4])

    first = edge_plane(0, 1, low2, volts2[:, 1:2])
    last = edge_plane(planes - 1, planes, volts2[:, planes - 2 : planes - 1], high2)
    step2 = jnp.concatenate([first, step2[:, 1 : planes - 1], last], axis=1)
    start2 = jnp.where(first_slice, start0, arrived2)
    ends2 = start2 + step2
    return ends2[None]


def solution(mesh):
    placed = (P("tm", None, "space", None, None), P("space", None, None), P("space", None, None))
    return jax.shard_map(
        steps,
        mesh=mesh,
        in_specs=placed,
        out_specs=P("tm", None, "space", None, None),
        check_vma=False,
    )
```

```python
import jax
import jax.numpy as jnp
from jax import lax
from jax.sharding import PartitionSpec as P


radau_nodes = [0.05710419611451768, 0.2768430136381238, 0.5835904323689168, 0.8602401356562195, 1.0]
slice_len = 0.6


def radau_table():
    table = []
    for m in range(5):
        row_values = []
        for j in range(5):
            polynom = [1.0]
            for i in range(5):
                if i != j:
                    factor = radau_nodes[j] - radau_nodes[i]
                    shifted = [0.0] + [value / factor for value in polynom]
                    scaled = [-radau_nodes[i] * value / factor for value in polynom] + [0.0]
                    polynom = [shifted[p] + scaled[p] for p in range(len(polynom) + 1)]
            integral = 0.0
            for p in range(len(polynom)):
                integral = integral + polynom[p] * radau_nodes[m] ** (p + 1) / (p + 1)
            row_values.append(integral)
        table.append(row_values)
    return table


def lookup(labels, values):
    total = jnp.zeros(labels.shape, jnp.float32)
    for level in range(len(values)):
        total = total + jnp.where(labels == level, values[level], 0.0).astype(jnp.float32)
    return total


def edge_pad(field, axis):
    size = field.shape[axis]
    low = lax.slice_in_dim(field, 0, 1, axis=axis)
    high = lax.slice_in_dim(field, size - 1, size, axis=axis)
    return jnp.concatenate([low, field, high], axis=axis)


def second(padded, axis):
    size = padded.shape[axis]
    upper = lax.slice_in_dim(padded, 2, size, axis=axis)
    lower = lax.slice_in_dim(padded, 0, size - 2, axis=axis)
    middle = lax.slice_in_dim(padded, 1, size - 1, axis=axis)
    return upper + lower - 2.0 * middle


def shift_space(block, forward):
    count = lax.axis_size("space")
    pairs = [(i, i + 1) for i in range(count - 1)]
    if not forward:
        pairs = [(t, s) for s, t in pairs]
    return lax.ppermute(block, "space", pairs)


def halos(volts):
    planes = volts.shape[-3]
    low = shift_space(volts[..., planes - 1 : planes, :, :], True)
    high = shift_space(volts[..., 0:1, :, :], False)
    return low, high


def laplacian(volts, low, high, conduct):
    padded = jnp.concatenate([low, volts, high], axis=-3)
    lap = conduct[0] * second(padded, volts.ndim - 3)
    lap = lap + conduct[1] * second(edge_pad(volts, volts.ndim - 2), volts.ndim - 2)
    lap = lap + conduct[2] * second(edge_pad(volts, volts.ndim - 1), volts.ndim - 1)
    return lap


def rates(states, lap, fast_g, slow_g, slow_tau):
    volt = states[..., 0, :, :, :]
    act = states[..., 1, :, :, :]
    inact = states[..., 2, :, :, :]
    slow = states[..., 3, :, :, :]
    current = (
        fast_g * act * act * act * inact * (volt - 1.0)
        + slow_g * slow * (volt + 0.2)
        + 0.3 * (volt + 0.1)
    )
    dvolt = lap - current
    dact = (jax.nn.sigmoid(8.0 * (volt - 0.2)) - act) / 0.5
    dinact = (jax.nn.sigmoid(-8.0 * (volt - 0.3)) - inact) / (
        1.0 + 3.0 * jax.nn.sigmoid(6.0 * (volt - 0.3))
    )
    dslow = (jax.nn.sigmoid(5.0 * (volt - 0.5)) - slow) / slow_tau
    return jnp.stack([dvolt, dact, dinact, dslow], axis=-4)


def increment(derivs, row):
    total = row[0] * derivs[0]
    for j in range(1, 5):
        total = total + row[j] * derivs[j]
    return slice_len * total


def edge_nodes(start, derivs, weights):
    total = weights[:, 0] * derivs[0][None]
    for j in range(1, 5):
        total = total + weights[:, j] * derivs[j][None]
    return start[None] + slice_len * total


def edge_rates(nodes, volts, plane, below, above, conduct, fast_g, slow_g, slow_tau):
    part = lambda c: c[plane : plane + 1]
    lap = laplacian(volts[:, plane : plane + 1], below, above, [part(c) for c in conduct])
    return rates(nodes[:, :, plane : plane + 1], lap, part(fast_g), part(slow_g), part(slow_tau))


def steps(guess, fibre, labels):
    table = radau_table()
    sums = [sum(row) for row in table]
    fast_g = lookup(labels, [4.0, 3.0, 3.5, 1.0])
    slow_g = lookup(labels, [0.6, 0.9, 0.75, 0.3])
    slow_tau = 4.0 * lookup(labels, [1.0, 1.5, 1.2, 3.0])
    conduct = [0.2 + 0.6 * (fibre == d).astype(jnp.float32) for d in range(3)]
    place = lax.axis_index("space")
    at_low = place == 0
    at_high = place == lax.axis_size("space") - 1
    first_slice = lax.axis_index("tm") == 0
    count = lax.axis_size("tm")
    tm_pairs = [(i, i + 1) for i in range(count - 1)]

    start0 = guess[0]
    volts0 = start0[0]
    planes = volts0.shape[0]

    low0, high0 = halos(volts0)
    low0 = jnp.where(at_low, volts0[:1], low0)
    high0 = jnp.where(at_high, volts0[planes - 1 :], high0)
    derivs0 = rates(start0, laplacian(volts0, low0, high0, conduct), fast_g, slow_g, slow_tau)
    ends0 = start0 + slice_len * (sums[4] * derivs0)
    derivs0, ends0 = lax.optimization_barrier((derivs0, ends0))
    arrived1 = lax.ppermute(ends0, "tm", tm_pairs)

    dv = derivs0[0]
    dlow, dhigh = halos(dv)
    nodes0 = jnp.stack([start0 + slice_len * (sums[m] * derivs0) for m in range(5)])
    volts1 = nodes0[:, 0]
    low1 = jnp.stack([low0 + slice_len * (sums[m] * dlow) for m in range(5)])
    high1 = jnp.stack([high0 + slice_len * (sums[m] * dhigh) for m in range(5)])
    low1 = jnp.where(at_low, volts1[:, :1], low1)
    high1 = jnp.where(at_high, volts1[:, planes - 1 :], high1)
    rough1 = rates(nodes0, laplacian(volts1, volts1[:, :1], volts1[:, planes - 1 :], conduct), fast_g, slow_g, slow_tau)
    inner1 = lax.optimization_barrier(increment(rough1, table[4]))
    first1 = edge_rates(nodes0, volts1, 0, low1, volts1[:, 1:2], conduct, fast_g, slow_g, slow_tau)
    last1 = edge_rates(
        nodes0, volts1, planes - 1, volts1[:, planes - 2 : planes - 1], high1, conduct, fast_g, slow_g, slow_tau
    )
    derivs1 = jnp.concatenate([first1, rough1[:, :, 1 : planes - 1], last1], axis=2)
    step1 = jnp.concatenate(
        [increment(first1, table[4]), inner1[:, 1 : planes - 1], increment(last1, table[4])], axis=1
    )
    start1 = jnp.where(first_slice, start0, arrived1)
    ends1 = start1 + step1
    arrived2 = lax.ppermute(ends1, "tm", tm_pairs)
    later_start, later_derivs, ends1 = lax.optimization_barrier((start1, derivs1, ends1))
    weights = jnp.array(table, jnp.float32)[:, :, None, None, None]
    top = edge_nodes(later_start[0, planes - 1 :], later_derivs[:, 0, planes - 1 :], weights)
    bottom = edge_nodes(later_start[0, :1], later_derivs[:, 0, :1], weights)
    low2 = shift_space(top, True)
    high2 = shift_space(bottom, False)
    nodes1 = edge_nodes(later_start, later_derivs, weights[..., None])

    volts2 = nodes1[:, 0]
    low2 = jnp.where(at_low, volts2[:, :1], low2)
    high2 = jnp.where(at_high, volts2[:, planes - 1 :], high2)
    rough = rates(nodes1, laplacian(volts2, volts2[:, :1], volts2[:, planes - 1 :], conduct), fast_g, slow_g, slow_tau)
    step2 = lax.optimization_barrier(increment(rough, table[4]))

    def edge_plane(lo, hi, below, above):
        part = lambda c: c[lo:hi]
        lap = laplacian(volts2[:, lo:hi], below, above, [part(c) for c in conduct])
        derivs = rates(nodes1[:, :, lo:hi], lap, part(fast_g), part(slow_g), part(slow_tau))
        return increment(derivs, table[4])

    first = edge_plane(0, 1, low2, volts2[:, 1:2])
    last = edge_plane(planes - 1, planes, volts2[:, planes - 2 : planes - 1], high2)
    step2 = jnp.concatenate([first, step2[:, 1 : planes - 1], last], axis=1)
    start2 = jnp.where(first_slice, start0, arrived2)
    ends2 = start2 + step2
    return ends2[None]


def solution(mesh):
    placed = (P("tm", None, "space", None, None), P("space", None, None), P("space", None, None))
    return jax.shard_map(
        steps,
        mesh=mesh,
        in_specs=placed,
        out_specs=P("tm", None, "space", None, None),
        check_vma=False,
    )
```

```python
import jax
import jax.numpy as jnp
from jax import lax
from jax.sharding import PartitionSpec as P


radau_nodes = [0.05710419611451768, 0.2768430136381238, 0.5835904323689168, 0.8602401356562195, 1.0]
slice_len = 0.6


def radau_table():
    table = []
    for m in range(5):
        row_values = []
        for j in range(5):
            polynom = [1.0]
            for i in range(5):
                if i != j:
                    factor = radau_nodes[j] - radau_nodes[i]
                    shifted = [0.0] + [value / factor for value in polynom]
                    scaled = [-radau_nodes[i] * value / factor for value in polynom] + [0.0]
                    polynom = [shifted[p] + scaled[p] for p in range(len(polynom) + 1)]
            integral = 0.0
            for p in range(len(polynom)):
                integral = integral + polynom[p] * radau_nodes[m] ** (p + 1) / (p + 1)
            row_values.append(integral)
        table.append(row_values)
    return table


def lookup(labels, values):
    total = jnp.zeros(labels.shape, jnp.float32)
    for level in range(len(values)):
        total = total + jnp.where(labels == level, values[level], 0.0).astype(jnp.float32)
    return total


def edge_pad(field, axis):
    size = field.shape[axis]
    low = lax.slice_in_dim(field, 0, 1, axis=axis)
    high = lax.slice_in_dim(field, size - 1, size, axis=axis)
    return jnp.concatenate([low, field, high], axis=axis)


def second(padded, axis):
    size = padded.shape[axis]
    upper = lax.slice_in_dim(padded, 2, size, axis=axis)
    lower = lax.slice_in_dim(padded, 0, size - 2, axis=axis)
    middle = lax.slice_in_dim(padded, 1, size - 1, axis=axis)
    return upper + lower - 2.0 * middle


def shift_space(block, forward):
    count = lax.axis_size("space")
    pairs = [(i, i + 1) for i in range(count - 1)]
    if not forward:
        pairs = [(t, s) for s, t in pairs]
    return lax.ppermute(block, "space", pairs)


def halos(volts):
    planes = volts.shape[-3]
    low = shift_space(volts[..., planes - 1 : planes, :, :], True)
    high = shift_space(volts[..., 0:1, :, :], False)
    return low, high


def laplacian(volts, low, high, conduct):
    padded = jnp.concatenate([low, volts, high], axis=-3)
    lap = conduct[0] * second(padded, volts.ndim - 3)
    lap = lap + conduct[1] * second(edge_pad(volts, volts.ndim - 2), volts.ndim - 2)
    lap = lap + conduct[2] * second(edge_pad(volts, volts.ndim - 1), volts.ndim - 1)
    return lap


def rates(states, lap, fast_g, slow_g, slow_tau):
    volt = states[..., 0, :, :, :]
    act = states[..., 1, :, :, :]
    inact = states[..., 2, :, :, :]
    slow = states[..., 3, :, :, :]
    current = (
        fast_g * act * act * act * inact * (volt - 1.0)
        + slow_g * slow * (volt + 0.2)
        + 0.3 * (volt + 0.1)
    )
    dvolt = lap - current
    dact = (jax.nn.sigmoid(8.0 * (volt - 0.2)) - act) / 0.5
    dinact = (jax.nn.sigmoid(-8.0 * (volt - 0.3)) - inact) / (
        1.0 + 3.0 * jax.nn.sigmoid(6.0 * (volt - 0.3))
    )
    dslow = (jax.nn.sigmoid(5.0 * (volt - 0.5)) - slow) / slow_tau
    return jnp.stack([dvolt, dact, dinact, dslow], axis=-4)


def increment(derivs, row):
    total = row[0] * derivs[0]
    for j in range(1, 5):
        total = total + row[j] * derivs[j]
    return slice_len * total


def edge_nodes(start, derivs, weights):
    total = weights[:, 0] * derivs[0][None]
    for j in range(1, 5):
        total = total + weights[:, j] * derivs[j][None]
    return start[None] + slice_len * total


def edge_rates(nodes, volts, plane, below, above, conduct, fast_g, slow_g, slow_tau):
    part = lambda c: c[plane : plane + 1]
    lap = laplacian(volts[:, plane : plane + 1], below, above, [part(c) for c in conduct])
    return rates(nodes[:, :, plane : plane + 1], lap, part(fast_g), part(slow_g), part(slow_tau))


def steps(guess, fibre, labels):
    table = radau_table()
    sums = [sum(row) for row in table]
    fast_g = lookup(labels, [4.0, 3.0, 3.5, 1.0])
    slow_g = lookup(labels, [0.6, 0.9, 0.75, 0.3])
    slow_tau = 4.0 * lookup(labels, [1.0, 1.5, 1.2, 3.0])
    conduct = [0.2 + 0.6 * (fibre == d).astype(jnp.float32) for d in range(3)]
    place = lax.axis_index("space")
    at_low = place == 0
    at_high = place == lax.axis_size("space") - 1
    first_slice = lax.axis_index("tm") == 0
    count = lax.axis_size("tm")
    tm_pairs = [(i, i + 1) for i in range(count - 1)]

    start0 = guess[0]
    volts0 = start0[0]
    planes = volts0.shape[0]

    low0, high0 = halos(volts0)
    low0 = jnp.where(at_low, volts0[:1], low0)
    high0 = jnp.where(at_high, volts0[planes - 1 :], high0)
    rough0 = rates(start0, laplacian(volts0, volts0[:1], volts0[planes - 1 :], conduct), fast_g, slow_g, slow_tau)
    rough0 = lax.optimization_barrier(rough0)
    first0 = edge_rates(start0[None], volts0[None], 0, low0[None], volts0[None, 1:2], conduct, fast_g, slow_g, slow_tau)[0]
    last0 = edge_rates(
        start0[None], volts0[None], planes - 1, volts0[None, planes - 2 : planes - 1], high0[None], conduct,
        fast_g, slow_g, slow_tau,
    )[0]
    derivs0 = jnp.concatenate([first0, rough0[:, 1 : planes - 1], last0], axis=1)
    ends0 = start0 + slice_len * (sums[4] * derivs0)
    first0, last0, ends0 = lax.optimization_barrier((first0, last0, ends0))
    derivs0 = jnp.concatenate([first0, rough0[:, 1 : planes - 1], last0], axis=1)
    arrived1 = lax.ppermute(ends0, "tm", tm_pairs)

    dv = derivs0[0]
    dlow, dhigh = halos(dv)
    nodes0 = jnp.stack([start0 + slice_len * (sums[m] * derivs0) for m in range(5)])
    volts1 = nodes0[:, 0]
    low1 = jnp.stack([low0 + slice_len * (sums[m] * dlow) for m in range(5)])
    high1 = jnp.stack([high0 + slice_len * (sums[m] * dhigh) for m in range(5)])
    low1 = jnp.where(at_low, volts1[:, :1], low1)
    high1 = jnp.where(at_high, volts1[:, planes - 1 :], high1)
    derivs1 = rates(nodes0, laplacian(volts1, low1, high1, conduct), fast_g, slow_g, slow_tau)
    step1 = lax.optimization_barrier(increment(derivs1, table[4]))
    start1 = jnp.where(first_slice, start0, arrived1)
    ends1 = start1 + step1
    arrived2 = lax.ppermute(ends1, "tm", tm_pairs)
    later_start, later_derivs, ends1 = lax.optimization_barrier((start1, derivs1, ends1))
    weights = jnp.array(table, jnp.float32)[:, :, None, None, None]
    top = edge_nodes(later_start[0, planes - 1 :], later_derivs[:, 0, planes - 1 :], weights)
    bottom = edge_nodes(later_start[0, :1], later_derivs[:, 0, :1], weights)
    low2 = shift_space(top, True)
    high2 = shift_space(bottom, False)
    nodes1 = edge_nodes(later_start, later_derivs, weights[..., None])

    volts2 = nodes1[:, 0]
    low2 = jnp.where(at_low, volts2[:, :1], low2)
    high2 = jnp.where(at_high, volts2[:, planes - 1 :], high2)
    rough = rates(nodes1, laplacian(volts2, volts2[:, :1], volts2[:, planes - 1 :], conduct), fast_g, slow_g, slow_tau)
    step2 = lax.optimization_barrier(increment(rough, table[4]))

    def edge_plane(lo, hi, below, above):
        part = lambda c: c[lo:hi]
        lap = laplacian(volts2[:, lo:hi], below, above, [part(c) for c in conduct])
        derivs = rates(nodes1[:, :, lo:hi], lap, part(fast_g), part(slow_g), part(slow_tau))
        return increment(derivs, table[4])

    first = edge_plane(0, 1, low2, volts2[:, 1:2])
    last = edge_plane(planes - 1, planes, volts2[:, planes - 2 : planes - 1], high2)
    step2 = jnp.concatenate([first, step2[:, 1 : planes - 1], last], axis=1)
    start2 = jnp.where(first_slice, start0, arrived2)
    ends2 = start2 + step2
    return ends2[None]


def solution(mesh):
    placed = (P("tm", None, "space", None, None), P("space", None, None), P("space", None, None))
    return jax.shard_map(
        steps,
        mesh=mesh,
        in_specs=placed,
        out_specs=P("tm", None, "space", None, None),
        check_vma=False,
    )
```
